256 devices in a mesh: species: 4 (over z_lo), mode: 4 (over y), space: 16 (over x, z_hi, core).
Axes of the slice: x: 4, y: 4, z: 8 (z_hi: 2, z_lo: 4; z = z_hi * 4 + z_lo), core: 2. Of those that a mesh axis runs over, the one named last changes fastest.
Arguments:
- distribution: float32 [8, 1024, 16, 512], P('species', 'mode', 'space'), may hold values from -6 to 6
- kernel: bfloat16 [2, 120, 120, 120], P(None, 'mode'), may hold values from -0.046875 to 0.046875
- pair_kind: int32 [8, 8], replicated, may hold values from 0 to 1
- low_map: int32 [120], replicated, may hold values from 0 to 448, as said below
- thermal_speed: float32 [8], P('species'), may hold values from 0.5 to 1
- relax_rate: float32 [8], P('species'), may hold values from 2 to 8
Outputs:
- updated: float32 [8, 1024, 16, 512], P('species', 'mode', 'space')
The draws below stay inside these ranges and needn't reach their ends.
Inputs may be any that keep to these rules, and one draw needn't show every extreme that they name: low_map lists each of the 120 modes whose degrees a, b, c sum to at most 7 exactly once, in some order; a mode's index is a * 8 * 8 + b * 8 + c.
All inputs are finite; a program needn't handle non-finite values.
Results may differ from the reference program's by a relative error of at most 0.0025.
Values may be sent and summed in bfloat16 or wider, within the bound.
No kernel may reach another device: no remote copies, remote signals or barrier semaphores. Data moves between devices by JAX's collectives and lax.ppermute only.
A program may use at most 128 MiB of HBM per device.

```python
import math
import jax
import jax.numpy as jnp
import numpy as np
from jax import lax

SPECIES = 8
NVX = 16
NVY = 8
NVZ = 8
MODES = 1024
DEG = 7
K = 120
NKIND = 2
NX = 16
NY = 256
NZ = 2
PLANE = 512


def draw_low_map(key, part):
    mode_table = np.array([degree_a * NVY * NVZ + degree_b * NVZ + degree_c for degree_a in range(DEG + 1) for degree_b in range(DEG + 1) for degree_c in range(DEG + 1) if degree_a + degree_b + degree_c <= DEG], dtype=np.int32)
    shuffled = jax.random.permutation(key, mode_table.shape[0])
    return jnp.asarray(mode_table)[shuffled].astype(jnp.int32)


def plant(drawn, stream_key, least, top_value):
    spot = [jax.random.randint(jax.random.fold_in(stream_key, axis), (), 0, length) for axis, length in enumerate(drawn.shape)]
    main_axis = drawn.shape.index(max(drawn.shape))
    beside = spot[:main_axis] + [(spot[main_axis] + 1) % drawn.shape[main_axis]] + spot[main_axis + 1:]
    return drawn.at[tuple(spot)].set(least).at[tuple(beside)].set(top_value)


def block_scale(own_key, dims, pieces, low, high):
    level, own = 1.0, jax.random.fold_in(own_key, 6)
    for position, blocks in pieces:
        draws = jnp.exp(jax.random.uniform(jax.random.fold_in(own, position), (blocks,), jnp.float32, low / len(pieces), high / len(pieces)))
        level = level * jnp.repeat(draws, dims[position] // blocks).reshape([-1 if axis == position else 1 for axis in range(len(dims))])
    return level


def centred(stream_key, extent, scale, reach, shards=(), kind=jnp.bfloat16):
    level = block_scale(stream_key, extent, shards, -0.22, 0.18) if shards else 1.0
    values = jax.random.normal(stream_key, extent, jnp.float32) * scale * level
    return jnp.minimum(jnp.maximum(values, -reach), reach).astype(kind)


def setup_inputs(seed: int = 0) -> dict:
    key_list = jax.random.split(jax.random.key(seed), 7)
    distribution = centred(key_list[0], (SPECIES, MODES, NX, PLANE), 1.0, 6.0, ((0, 4), (1, 4), (2, 16)), jnp.float32)
    kernel = centred(key_list[1], (NKIND, K, K, K), (K * K) ** -0.5, 0.046875, ((1, 4),))
    pair_kind = plant(jax.random.randint(key_list[2], (SPECIES, SPECIES), 0, NKIND), jax.random.fold_in(key_list[2], 1), 0, NKIND - 1).astype(jnp.int32)
    low_map = draw_low_map(jax.random.fold_in(key_list[6], 71), 0)
    thermal_speed = jnp.clip(jnp.exp(math.log(1.0) - 0.6931472 * jax.random.uniform(key_list[4], (SPECIES,), jnp.float32) ** block_scale(key_list[4], (SPECIES,), ((0, 4),), -0.2, 0.2)), 0.5, 1.0)
    relax_rate = jnp.clip(jnp.exp(math.log(8.0) - 1.3862944 * jax.random.uniform(key_list[5], (SPECIES,), jnp.float32) ** block_scale(key_list[5], (SPECIES,), ((0, 4),), -0.2, 0.2)), 2.0, 8.0)
    return {"distribution": distribution, "kernel": kernel, "pair_kind": pair_kind, "low_map": low_map, "thermal_speed": thermal_speed, "relax_rate": relax_rate}


nu_step = 0.0625
dt_step = 0.05
bound_x = 6.7
bound_y = 4.2
bound_z = 4.2

def flux_from_padded(padded, axis_dim, first_degree):
    axis_count = padded.shape[axis_dim] - 2
    dims_shape = [1] * padded.ndim
    dims_shape[axis_dim] = axis_count
    degree = (first_degree + jnp.arange(axis_count)).astype(jnp.float32).reshape(dims_shape)
    below_part = lax.slice_in_dim(padded, 0, axis_count, axis=axis_dim)
    above_part = lax.slice_in_dim(padded, 2, axis_count + 2, axis=axis_dim)
    return jnp.sqrt(degree + 1.0) * above_part + jnp.sqrt(degree) * below_part

def degree_flux(phase_field, axis_dim):
    widths = [(0, 0)] * phase_field.ndim
    widths[axis_dim] = (1, 1)
    return flux_from_padded(jnp.pad(phase_field, widths), axis_dim, 0)

def rusanov(phase_field, up_field, down_field, up_flux, down_flux, speed_bound):
    return 0.5 * (up_flux - down_flux) - 0.5 * speed_bound * (up_field - 2.0 * phase_field + down_field)

def periodic_term(phase_field, axis_deg, axis_cell, speed_bound):
    flux_dir = degree_flux(phase_field, axis_deg)
    return rusanov(phase_field, jnp.roll(phase_field, -1, axis_cell), jnp.roll(phase_field, 1, axis_cell), jnp.roll(flux_dir, -1, axis_cell), jnp.roll(flux_dir, 1, axis_cell), speed_bound)

def reference(distribution, kernel, pair_kind, low_map, thermal_speed, relax_rate):
    phase_field = distribution.reshape(SPECIES, NVX, NVY, NVZ, NX, NZ, NY)
    widths = [(0, 0)] * 7
    widths[4] = (1, 1)
    flux_x = degree_flux(phase_field, 1)
    wide_field = jnp.pad(phase_field, widths)
    wide_flux = jnp.pad(flux_x, widths)
    x_term = rusanov(phase_field, lax.slice_in_dim(wide_field, 2, NX + 2, axis=4), lax.slice_in_dim(wide_field, 0, NX, axis=4), lax.slice_in_dim(wide_flux, 2, NX + 2, axis=4), lax.slice_in_dim(wide_flux, 0, NX, axis=4), bound_x)
    y_term = periodic_term(phase_field, 2, 6, bound_y)
    z_term = periodic_term(phase_field, 3, 5, bound_z)
    stream = x_term + y_term + z_term
    advected = phase_field - nu_step * thermal_speed.reshape(SPECIES, 1, 1, 1, 1, 1, 1) * stream
    flat_dist = distribution.reshape(SPECIES, MODES, NX, PLANE)
    low_block = flat_dist[:, low_map].astype(jnp.bfloat16)
    kernel_f32 = kernel.astype(jnp.float32)
    chooser = jnp.stack([(pair_kind == kind_index).astype(jnp.float32) for kind_index in range(NKIND)])

    def row_collide(piece):
        values = piece.astype(jnp.float32)
        summed = jnp.zeros((SPECIES, K, PLANE), jnp.float32)
        for kind_index in range(NKIND):
            partner_sum = jnp.einsum('sr,rlc->slc', chooser[kind_index], values, precision=lax.Precision.HIGHEST)
            mixed_terms = jnp.einsum('nkl,skc->snlc', kernel_f32[kind_index], values, precision=lax.Precision.HIGHEST)
            summed = summed + jnp.einsum('snlc,slc->snc', mixed_terms, partner_sum, precision=lax.Precision.HIGHEST)
        return summed
    row_results = lax.map(row_collide, jnp.moveaxis(low_block, 2, 0))
    gained = jnp.moveaxis(row_results, 0, 2)
    collide = jnp.zeros((SPECIES, MODES, NX, PLANE), jnp.float32).at[:, low_map].set(gained)
    degree_total = (jnp.arange(NVX)[:, None, None] + jnp.arange(NVY)[None, :, None] + jnp.arange(NVZ)[None, None, :]).reshape(MODES)
    high_mask = (degree_total > DEG).astype(jnp.float32).reshape(1, MODES, 1, 1)
    collide = collide - high_mask * relax_rate.reshape(SPECIES, 1, 1, 1) * flat_dist
    return advected.reshape(SPECIES, MODES, NX, PLANE) + dt_step * collide
```

```python
import jax
import jax.numpy as jnp
from jax import lax
from jax.experimental import pallas as pl
from jax.sharding import PartitionSpec as P

NVY = 8
NVZ = 8
DEG = 7
NKIND = 2
NY = 256
NZ = 2
PAD = 128

nu_step = 0.0625
dt_step = 0.05
bound_x = 6.7
bound_y = 4.2
bound_z = 4.2

INTERPRET = False


def flux_from_padded(padded, axis_dim, first_degree):
    axis_count = padded.shape[axis_dim] - 2
    dims_shape = [1] * padded.ndim
    dims_shape[axis_dim] = axis_count
    degree = (first_degree + jnp.arange(axis_count)).astype(jnp.float32).reshape(dims_shape)
    below_part = lax.slice_in_dim(padded, 0, axis_count, axis=axis_dim)
    above_part = lax.slice_in_dim(padded, 2, axis_count + 2, axis=axis_dim)
    return jnp.sqrt(degree + 1.0) * above_part + jnp.sqrt(degree) * below_part


def degree_flux(phase_field, axis_dim):
    widths = [(0, 0)] * phase_field.ndim
    widths[axis_dim] = (1, 1)
    return flux_from_padded(jnp.pad(phase_field, widths), axis_dim, 0)


def rusanov(phase_field, up_field, down_field, up_flux, down_flux, speed_bound):
    return 0.5 * (up_flux - down_flux) - 0.5 * speed_bound * (
        up_field - 2.0 * phase_field + down_field
    )


def periodic_term(phase_field, axis_deg, axis_cell, speed_bound):
    flux_dir = degree_flux(phase_field, axis_deg)
    return rusanov(
        phase_field,
        jnp.roll(phase_field, -1, axis_cell),
        jnp.roll(phase_field, 1, axis_cell),
        jnp.roll(flux_dir, -1, axis_cell),
        jnp.roll(flux_dir, 1, axis_cell),
        speed_bound,
    )


def collide_body(k_ref, r_ref, l_ref, o_ref):
    def body(n, carry):
        z = jnp.dot(k_ref[n], r_ref[...], preferred_element_type=jnp.float32)
        o_ref[pl.ds(n, 1), :] = jnp.sum(z * l_ref[...], axis=0, keepdims=True)
        return carry

    lax.fori_loop(0, k_ref.shape[0], body, 0)


def collide_call(kcat, rhs, lmat):
    return pl.pallas_call(
        collide_body,
        out_shape=jax.ShapeDtypeStruct((kcat.shape[0], rhs.shape[1]), jnp.float32),
        interpret=INTERPRET,
    )(kcat, rhs, lmat)


def shift_permutes(values, axis, holders, count, toward):
    received = []
    for shift in range(1, count):
        if toward:
            pairs = [((h - shift) % count, h) for h in holders]
        else:
            pairs = [(h, (h + shift) % count) for h in holders]
        received.append((shift, lax.ppermute(values, axis, pairs)))
    return received


def per_device(distribution, kernel, pair_kind, low_map, thermal_speed, relax_rate):
    own_count, mode_count, row_count, plane_cells = distribution.shape
    per_vx = mode_count // (NVY * NVZ)
    mode_devs = lax.axis_size("mode")
    species_devs = lax.axis_size("species")
    space_devs = lax.axis_size("space")
    mode_id = lax.axis_index("mode")
    first_vx = mode_id * per_vx
    low_count = low_map.shape[0]
    out_rows = kernel.shape[1]
    species_all = own_count * species_devs

    phase_field = distribution.reshape(own_count, per_vx, NVY, NVZ, row_count, NZ, NY)
    below = lax.ppermute(
        phase_field[:, per_vx - 1 :], "mode", [(i, i + 1) for i in range(mode_devs - 1)]
    )
    above = lax.ppermute(phase_field[:, :1], "mode", [(i + 1, i) for i in range(mode_devs - 1)])
    flux_x = flux_from_padded(jnp.concatenate([below, phase_field, above], axis=1), 1, first_vx)
    up_part = 0.5 * flux_x - 0.5 * bound_x * phase_field
    down_part = -0.5 * flux_x - 0.5 * bound_x * phase_field
    from_next = lax.ppermute(
        up_part[:, :, :, :, :1], "space", [(i + 1, i) for i in range(space_devs - 1)]
    )
    from_prev = lax.ppermute(
        down_part[:, :, :, :, row_count - 1 :], "space", [(i, i + 1) for i in range(space_devs - 1)]
    )
    up_all = jnp.concatenate([up_part[:, :, :, :, 1:], from_next], axis=4)
    down_all = jnp.concatenate([from_prev, down_part[:, :, :, :, : row_count - 1]], axis=4)
    x_term = up_all + down_all + bound_x * phase_field
    y_term = periodic_term(phase_field, 2, 6, bound_y)
    z_term = periodic_term(phase_field, 3, 5, bound_z)
    stream = x_term + y_term + z_term
    advected = phase_field - nu_step * thermal_speed.reshape(own_count, 1, 1, 1, 1, 1, 1) * stream

    cell_count = row_count * plane_cells
    block_cells = cell_count // species_devs
    flat_dist = distribution.reshape(own_count, mode_count, cell_count)
    local_index = low_map - mode_id * mode_count
    owned = (local_index >= 0) & (local_index < mode_count)
    clipped = jnp.clip(local_index, 0, mode_count - 1)
    picked = jnp.where(owned[None, :, None], jnp.take(flat_dist, clipped, axis=1), 0.0).astype(
        jnp.bfloat16
    )
    picked = picked.reshape(own_count, low_count, species_devs, block_cells)
    spread = lax.all_to_all(picked, "species", 2, 0, tiled=True)
    holders = [h for h in range(mode_devs) if h * per_vx <= DEG]
    low_all = spread
    for _, got in shift_permutes(spread, "mode", holders, mode_devs, False):
        low_all = low_all + got
    low_all = low_all.reshape(species_all, low_count, block_cells).astype(jnp.float32)

    chooser = jnp.stack([(pair_kind == k).astype(jnp.float32) for k in range(NKIND)])
    partner = jnp.einsum("ksr,rlc->klsc", chooser, low_all, precision=lax.Precision.HIGHEST)
    part_hi = partner.astype(jnp.bfloat16)
    part_lo = (partner - part_hi.astype(jnp.float32)).astype(jnp.bfloat16)
    rhs = jnp.stack([piece for k in range(NKIND) for piece in (part_hi[k], part_lo[k])])
    rhs = jnp.pad(rhs, ((0, 0), (0, PAD - low_count), (0, 0), (0, 0)))
    rhs = rhs.reshape(2 * NKIND * PAD, species_all * block_cells)
    lmat = jnp.pad(jnp.moveaxis(low_all, 1, 0), ((0, PAD - low_count), (0, 0), (0, 0)))
    lmat = lmat.reshape(PAD, species_all * block_cells)
    kpad = jnp.pad(kernel, ((0, 0), (0, 0), (0, PAD - low_count), (0, PAD - low_count)))
    kcat = jnp.concatenate([kpad[k] for k in range(NKIND) for _ in range(2)], axis=-1)
    gained = collide_call(kcat, rhs, lmat)

    gained = gained.reshape(out_rows, species_devs, own_count, block_cells)
    gathered = lax.all_to_all(gained, "species", 1, 3, tiled=True)
    gathered = gathered.reshape(out_rows, own_count, cell_count)
    pieces = [None] * mode_devs
    pieces[0] = gathered
    for shift, got in shift_permutes(gathered, "mode", holders, mode_devs, True):
        pieces[shift] = got
    stacked = jnp.stack(pieces)
    by_source = jnp.take(stacked, (mode_id - jnp.arange(mode_devs)) % mode_devs, axis=0)
    all_gained = by_source.reshape(mode_devs * out_rows, own_count, cell_count)

    local_modes = mode_id * mode_count + jnp.arange(mode_count)
    match = low_map[None, :] == local_modes[:, None]
    inverse = jnp.argmax(match, axis=1)
    coll_low = jnp.moveaxis(jnp.take(all_gained, inverse, axis=0), 0, 1)
    vx_degree = first_vx + jnp.arange(per_vx)
    degree_total = (
        vx_degree[:, None, None] + jnp.arange(NVY)[None, :, None] + jnp.arange(NVZ)[None, None, :]
    ).reshape(1, mode_count, 1)
    collide = jnp.where(
        degree_total > DEG, -relax_rate.reshape(own_count, 1, 1) * flat_dist, coll_low
    )
    return advected.reshape(
        own_count, mode_count, row_count, plane_cells
    ) + dt_step * collide.reshape(own_count, mode_count, row_count, plane_cells)


def solution(mesh):
    in_specs = (
        P("species", "mode", "space", None),
        P(None, "mode", None, None),
        P(),
        P(),
        P("species"),
        P("species"),
    )
    out_specs = P("species", "mode", "space", None)
    return jax.shard_map(
        per_device, mesh=mesh, in_specs=in_specs, out_specs=out_specs, check_vma=False
    )
```

```python
import jax
import jax.numpy as jnp
from jax import lax
from jax.experimental import pallas as pl
from jax.sharding import PartitionSpec as P

NVY = 8
NVZ = 8
DEG = 7
NKIND = 2
NY = 256
NZ = 2
PAD = 128

nu_step = 0.0625
dt_step = 0.05
bound_x = 6.7
bound_y = 4.2
bound_z = 4.2

INTERPRET = False


def flux_from_padded(padded, axis_dim, first_degree):
    axis_count = padded.shape[axis_dim] - 2
    dims_shape = [1] * padded.ndim
    dims_shape[axis_dim] = axis_count
    degree = (first_degree + jnp.arange(axis_count)).astype(jnp.float32).reshape(dims_shape)
    below_part = lax.slice_in_dim(padded, 0, axis_count, axis=axis_dim)
    above_part = lax.slice_in_dim(padded, 2, axis_count + 2, axis=axis_dim)
    return jnp.sqrt(degree + 1.0) * above_part + jnp.sqrt(degree) * below_part


def degree_flux(phase_field, axis_dim):
    widths = [(0, 0)] * phase_field.ndim
    widths[axis_dim] = (1, 1)
    return flux_from_padded(jnp.pad(phase_field, widths), axis_dim, 0)


def rusanov(phase_field, up_field, down_field, up_flux, down_flux, speed_bound):
    return 0.5 * (up_flux - down_flux) - 0.5 * speed_bound * (
        up_field - 2.0 * phase_field + down_field
    )


def periodic_term(phase_field, axis_deg, axis_cell, speed_bound):
    flux_dir = degree_flux(phase_field, axis_deg)
    return rusanov(
        phase_field,
        jnp.roll(phase_field, -1, axis_cell),
        jnp.roll(phase_field, 1, axis_cell),
        jnp.roll(flux_dir, -1, axis_cell),
        jnp.roll(flux_dir, 1, axis_cell),
        speed_bound,
    )


def collide_body(k_ref, r_ref, l_ref, o_ref):
    def body(n, carry):
        z = jnp.dot(k_ref[n], r_ref[...], preferred_element_type=jnp.float32)
        o_ref[pl.ds(n, 1), :] = jnp.sum(z * l_ref[...], axis=0, keepdims=True)
        return carry

    lax.fori_loop(0, k_ref.shape[0], body, 0)


def collide_call(kcat, rhs, lmat):
    return pl.pallas_call(
        collide_body,
        out_shape=jax.ShapeDtypeStruct((kcat.shape[0], rhs.shape[1]), jnp.float32),
        interpret=INTERPRET,
    )(kcat, rhs, lmat)


def shift_permutes(values, axis, holders, count, toward):
    received = []
    for shift in range(1, count):
        if toward:
            pairs = [((h - shift) % count, h) for h in holders]
        else:
            pairs = [(h, (h + shift) % count) for h in holders]
        received.append((shift, lax.ppermute(values, axis, pairs)))
    return received


def species_exchange(values, split_axis, concat_axis):
    count = lax.axis_size("species")
    me = lax.axis_index("species")
    pieces = [lax.dynamic_slice_in_dim(values, me, 1, axis=split_axis)]
    for shift in range(1, count):
        chunk = lax.dynamic_slice_in_dim(values, (me + shift) % count, 1, axis=split_axis)
        pieces.append(
            lax.ppermute(chunk, "species", [(i, (i + shift) % count) for i in range(count)])
        )
    stacked = jnp.stack(pieces)
    by_source = jnp.take(stacked, (me - jnp.arange(count)) % count, axis=0)
    by_source = jnp.moveaxis(by_source, 0, concat_axis)
    shape = list(values.shape)
    shape[split_axis] = 1
    shape[concat_axis] *= count
    merged = by_source.reshape(
        by_source.shape[:concat_axis]
        + (count * by_source.shape[concat_axis + 1],)
        + by_source.shape[concat_axis + 2 :]
    )
    return merged.reshape(shape)


def per_device(distribution, kernel, pair_kind, low_map, thermal_speed, relax_rate):
    own_count, mode_count, row_count, plane_cells = distribution.shape
    per_vx = mode_count // (NVY * NVZ)
    mode_devs = lax.axis_size("mode")
    species_devs = lax.axis_size("species")
    space_devs = lax.axis_size("space")
    mode_id = lax.axis_index("mode")
    first_vx = mode_id * per_vx
    low_count = low_map.shape[0]
    out_rows = kernel.shape[1]
    species_all = own_count * species_devs

    phase_field = distribution.reshape(own_count, per_vx, NVY, NVZ, row_count, NZ, NY)
    below = lax.ppermute(
        phase_field[:, per_vx - 1 :], "mode", [(i, i + 1) for i in range(mode_devs - 1)]
    )
    above = lax.ppermute(phase_field[:, :1], "mode", [(i + 1, i) for i in range(mode_devs - 1)])
    flux_x = flux_from_padded(jnp.concatenate([below, phase_field, above], axis=1), 1, first_vx)
    up_part = 0.5 * flux_x - 0.5 * bound_x * phase_field
    down_part = -0.5 * flux_x - 0.5 * bound_x * phase_field
    from_next = lax.ppermute(
        up_part[:, :, :, :, :1], "space", [(i + 1, i) for i in range(space_devs - 1)]
    )
    from_prev = lax.ppermute(
        down_part[:, :, :, :, row_count - 1 :], "space", [(i, i + 1) for i in range(space_devs - 1)]
    )
    up_all = jnp.concatenate([up_part[:, :, :, :, 1:], from_next], axis=4)
    down_all = jnp.concatenate([from_prev, down_part[:, :, :, :, : row_count - 1]], axis=4)
    x_term = up_all + down_all + bound_x * phase_field
    y_term = periodic_term(phase_field, 2, 6, bound_y)
    z_term = periodic_term(phase_field, 3, 5, bound_z)
    stream = x_term + y_term + z_term
    advected = phase_field - nu_step * thermal_speed.reshape(own_count, 1, 1, 1, 1, 1, 1) * stream

    cell_count = row_count * plane_cells
    block_cells = cell_count // species_devs
    flat_dist = distribution.reshape(own_count, mode_count, cell_count)
    local_index = low_map - mode_id * mode_count
    owned = (local_index >= 0) & (local_index < mode_count)
    clipped = jnp.clip(local_index, 0, mode_count - 1)
    picked = jnp.where(owned[None, :, None], jnp.take(flat_dist, clipped, axis=1), 0.0).astype(
        jnp.bfloat16
    )
    picked = picked.reshape(own_count, low_count, species_devs, block_cells)
    spread = species_exchange(picked, 2, 0)
    holders = [h for h in range(mode_devs) if h * per_vx <= DEG]
    low_all = spread
    for _, got in shift_permutes(spread, "mode", holders, mode_devs, False):
        low_all = low_all + got
    low_all = low_all.reshape(species_all, low_count, block_cells).astype(jnp.float32)

    chooser = jnp.stack([(pair_kind == k).astype(jnp.float32) for k in range(NKIND)])
    partner = jnp.einsum("ksr,rlc->klsc", chooser, low_all, precision=lax.Precision.HIGHEST)
    part_hi = partner.astype(jnp.bfloat16)
    part_lo = (partner - part_hi.astype(jnp.float32)).astype(jnp.bfloat16)
    rhs = jnp.stack([piece for k in range(NKIND) for piece in (part_hi[k], part_lo[k])])
    rhs = jnp.pad(rhs, ((0, 0), (0, PAD - low_count), (0, 0), (0, 0)))
    rhs = rhs.reshape(2 * NKIND * PAD, species_all * block_cells)
    lmat = jnp.pad(jnp.moveaxis(low_all, 1, 0), ((0, PAD - low_count), (0, 0), (0, 0)))
    lmat = lmat.reshape(PAD, species_all * block_cells)
    kpad = jnp.pad(kernel, ((0, 0), (0, 0), (0, PAD - low_count), (0, PAD - low_count)))
    kcat = jnp.concatenate([kpad[k] for k in range(NKIND) for _ in range(2)], axis=-1)
    gained = collide_call(kcat, rhs, lmat)

    gained = gained.reshape(out_rows, species_devs, own_count, block_cells)
    gathered = species_exchange(gained, 1, 3)
    gathered = gathered.reshape(out_rows, own_count, cell_count)
    pieces = [None] * mode_devs
    pieces[0] = gathered
    for shift, got in shift_permutes(gathered, "mode", holders, mode_devs, True):
        pieces[shift] = got
    stacked = jnp.stack(pieces)
    by_source = jnp.take(stacked, (mode_id - jnp.arange(mode_devs)) % mode_devs, axis=0)
    all_gained = by_source.reshape(mode_devs * out_rows, own_count, cell_count)

    local_modes = mode_id * mode_count + jnp.arange(mode_count)
    match = low_map[None, :] == local_modes[:, None]
    inverse = jnp.argmax(match, axis=1)
    coll_low = jnp.moveaxis(jnp.take(all_gained, inverse, axis=0), 0, 1)
    vx_degree = first_vx + jnp.arange(per_vx)
    degree_total = (
        vx_degree[:, None, None] + jnp.arange(NVY)[None, :, None] + jnp.arange(NVZ)[None, None, :]
    ).reshape(1, mode_count, 1)
    collide = jnp.where(
        degree_total > DEG, -relax_rate.reshape(own_count, 1, 1) * flat_dist, coll_low
    )
    return advected.reshape(
        own_count, mode_count, row_count, plane_cells
    ) + dt_step * collide.reshape(own_count, mode_count, row_count, plane_cells)


def solution(mesh):
    in_specs = (
        P("species", "mode", "space", None),
        P(None, "mode", None, None),
        P(),
        P(),
        P("species"),
        P("species"),
    )
    out_specs = P("species", "mode", "space", None)
    return jax.shard_map(
        per_device, mesh=mesh, in_specs=in_specs, out_specs=out_specs, check_vma=False
    )
```

```python
import jax
import jax.numpy as jnp
from jax import lax
from jax.experimental import pallas as pl
from jax.sharding import PartitionSpec as P

NVY = 8
NVZ = 8
DEG = 7
NKIND = 2
NY = 256
NZ = 2
PAD = 128
ROW_CHUNK = 10

nu_step = 0.0625
dt_step = 0.05
bound_x = 6.7
bound_y = 4.2
bound_z = 4.2

INTERPRET = False


def flux_from_padded(padded, axis_dim, first_degree):
    axis_count = padded.shape[axis_dim] - 2
    dims_shape = [1] * padded.ndim
    dims_shape[axis_dim] = axis_count
    degree = (first_degree + jnp.arange(axis_count)).astype(jnp.float32).reshape(dims_shape)
    below_part = lax.slice_in_dim(padded, 0, axis_count, axis=axis_dim)
    above_part = lax.slice_in_dim(padded, 2, axis_count + 2, axis=axis_dim)
    return jnp.sqrt(degree + 1.0) * above_part + jnp.sqrt(degree) * below_part


def degree_flux(phase_field, axis_dim):
    widths = [(0, 0)] * phase_field.ndim
    widths[axis_dim] = (1, 1)
    return flux_from_padded(jnp.pad(phase_field, widths), axis_dim, 0)


def rusanov(phase_field, up_field, down_field, up_flux, down_flux, speed_bound):
    return 0.5 * (up_flux - down_flux) - 0.5 * speed_bound * (
        up_field - 2.0 * phase_field + down_field
    )


def periodic_term(phase_field, axis_deg, axis_cell, speed_bound):
    flux_dir = degree_flux(phase_field, axis_deg)
    return rusanov(
        phase_field,
        jnp.roll(phase_field, -1, axis_cell),
        jnp.roll(phase_field, 1, axis_cell),
        jnp.roll(flux_dir, -1, axis_cell),
        jnp.roll(flux_dir, 1, axis_cell),
        speed_bound,
    )


def collide_body(k_ref, r_ref, l_ref, o_ref):
    rows, depth, width = k_ref.shape
    chunk = ROW_CHUNK

    def body(step, carry):
        first = step * chunk
        block = k_ref[pl.ds(first, chunk)].reshape(chunk * depth, width)
        z = jnp.dot(block, r_ref[...], preferred_element_type=jnp.float32)
        for i in range(chunk):
            part = z[i * depth : (i + 1) * depth] * l_ref[...]
            o_ref[pl.ds(first + i, 1), :] = jnp.sum(part, axis=0, keepdims=True)
        return carry

    lax.fori_loop(0, rows // chunk, body, 0)


def collide_call(kcat, rhs, lmat):
    return pl.pallas_call(
        collide_body,
        out_shape=jax.ShapeDtypeStruct((kcat.shape[0], rhs.shape[1]), jnp.float32),
        interpret=INTERPRET,
    )(kcat, rhs, lmat)


def shift_permutes(values, axis, holders, count, toward):
    received = []
    for shift in range(1, count):
        if toward:
            pairs = [((h - shift) % count, h) for h in holders]
        else:
            pairs = [(h, (h + shift) % count) for h in holders]
        received.append((shift, lax.ppermute(values, axis, pairs)))
    return received


def per_device(distribution, kernel, pair_kind, low_map, thermal_speed, relax_rate):
    own_count, mode_count, row_count, plane_cells = distribution.shape
    per_vx = mode_count // (NVY * NVZ)
    mode_devs = lax.axis_size("mode")
    species_devs = lax.axis_size("species")
    space_devs = lax.axis_size("space")
    mode_id = lax.axis_index("mode")
    first_vx = mode_id * per_vx
    low_count = low_map.shape[0]
    out_rows = kernel.shape[1]
    species_all = own_count * species_devs

    phase_field = distribution.reshape(own_count, per_vx, NVY, NVZ, row_count, NZ, NY)
    below = lax.ppermute(
        phase_field[:, per_vx - 1 :], "mode", [(i, i + 1) for i in range(mode_devs - 1)]
    )
    above = lax.ppermute(phase_field[:, :1], "mode", [(i + 1, i) for i in range(mode_devs - 1)])
    flux_x = flux_from_padded(jnp.concatenate([below, phase_field, above], axis=1), 1, first_vx)
    up_part = 0.5 * flux_x - 0.5 * bound_x * phase_field
    down_part = -0.5 * flux_x - 0.5 * bound_x * phase_field
    from_next = lax.ppermute(
        up_part[:, :, :, :, :1], "space", [(i + 1, i) for i in range(space_devs - 1)]
    )
    from_prev = lax.ppermute(
        down_part[:, :, :, :, row_count - 1 :], "space", [(i, i + 1) for i in range(space_devs - 1)]
    )
    up_all = jnp.concatenate([up_part[:, :, :, :, 1:], from_next], axis=4)
    down_all = jnp.concatenate([from_prev, down_part[:, :, :, :, : row_count - 1]], axis=4)
    x_term = up_all + down_all + bound_x * phase_field
    y_term = periodic_term(phase_field, 2, 6, bound_y)
    z_term = periodic_term(phase_field, 3, 5, bound_z)
    stream = x_term + y_term + z_term
    advected = phase_field - nu_step * thermal_speed.reshape(own_count, 1, 1, 1, 1, 1, 1) * stream

    cell_count = row_count * plane_cells
    block_cells = cell_count // species_devs
    flat_dist = distribution.reshape(own_count, mode_count, cell_count)
    local_index = low_map - mode_id * mode_count
    owned = (local_index >= 0) & (local_index < mode_count)
    clipped = jnp.clip(local_index, 0, mode_count - 1)
    picked = jnp.where(owned[None, :, None], jnp.take(flat_dist, clipped, axis=1), 0.0).astype(
        jnp.bfloat16
    )
    picked = picked.reshape(own_count, low_count, species_devs, block_cells)
    spread = lax.all_to_all(picked, "species", 2, 0, tiled=True)
    holders = [h for h in range(mode_devs) if h * per_vx <= DEG]
    low_all = spread
    for _, got in shift_permutes(spread, "mode", holders, mode_devs, False):
        low_all = low_all + got
    low_all = low_all.reshape(species_all, low_count, block_cells).astype(jnp.float32)

    chooser = jnp.stack([(pair_kind == k).astype(jnp.float32) for k in range(NKIND)])
    partner = jnp.einsum("ksr,rlc->klsc", chooser, low_all, precision=lax.Precision.HIGHEST)
    part_hi = partner.astype(jnp.bfloat16)
    part_lo = (partner - part_hi.astype(jnp.float32)).astype(jnp.bfloat16)
    rhs = jnp.stack([piece for k in range(NKIND) for piece in (part_hi[k], part_lo[k])])
    rhs = jnp.pad(rhs, ((0, 0), (0, PAD - low_count), (0, 0), (0, 0)))
    rhs = rhs.reshape(2 * NKIND * PAD, species_all * block_cells)
    lmat = jnp.pad(jnp.moveaxis(low_all, 1, 0), ((0, PAD - low_count), (0, 0), (0, 0)))
    lmat = lmat.reshape(PAD, species_all * block_cells)
    kpad = jnp.pad(kernel, ((0, 0), (0, 0), (0, PAD - low_count), (0, PAD - low_count)))
    kcat = jnp.concatenate([kpad[k] for k in range(NKIND) for _ in range(2)], axis=-1)
    gained = collide_call(kcat, rhs, lmat)

    gained = gained.reshape(out_rows, species_devs, own_count, block_cells)
    gathered = lax.all_to_all(gained, "species", 1, 3, tiled=True)
    gathered = gathered.reshape(out_rows, own_count, cell_count)
    pieces = [None] * mode_devs
    pieces[0] = gathered
    for shift, got in shift_permutes(gathered, "mode", holders, mode_devs, True):
        pieces[shift] = got
    stacked = jnp.stack(pieces)
    by_source = jnp.take(stacked, (mode_id - jnp.arange(mode_devs)) % mode_devs, axis=0)
    all_gained = by_source.reshape(mode_devs * out_rows, own_count, cell_count)

    local_modes = mode_id * mode_count + jnp.arange(mode_count)
    match = low_map[None, :] == local_modes[:, None]
    inverse = jnp.argmax(match, axis=1)
    coll_low = jnp.moveaxis(jnp.take(all_gained, inverse, axis=0), 0, 1)
    vx_degree = first_vx + jnp.arange(per_vx)
    degree_total = (
        vx_degree[:, None, None] + jnp.arange(NVY)[None, :, None] + jnp.arange(NVZ)[None, None, :]
    ).reshape(1, mode_count, 1)
    collide = jnp.where(
        degree_total > DEG, -relax_rate.reshape(own_count, 1, 1) * flat_dist, coll_low
    )
    return advected.reshape(
        own_count, mode_count, row_count, plane_cells
    ) + dt_step * collide.reshape(own_count, mode_count, row_count, plane_cells)


def solution(mesh):
    in_specs = (
        P("species", "mode", "space", None),
        P(None, "mode", None, None),
        P(),
        P(),
        P("species"),
        P("species"),
    )
    out_specs = P("species", "mode", "space", None)
    return jax.shard_map(
        per_device, mesh=mesh, in_specs=in_specs, out_specs=out_specs, check_vma=False
    )
```

```python
import jax
import jax.numpy as jnp
from jax import lax
from jax.experimental import pallas as pl
from jax.sharding import PartitionSpec as P

NVY = 8
NVZ = 8
DEG = 7
NKIND = 2
NY = 256
NZ = 2
PAD = 128
ROW_CHUNK = 10

nu_step = 0.0625
dt_step = 0.05
bound_x = 6.7
bound_y = 4.2
bound_z = 4.2

INTERPRET = False


def flux_from_padded(padded, axis_dim, first_degree):
    axis_count = padded.shape[axis_dim] - 2
    dims_shape = [1] * padded.ndim
    dims_shape[axis_dim] = axis_count
    degree = (first_degree + jnp.arange(axis_count)).astype(jnp.float32).reshape(dims_shape)
    below_part = lax.slice_in_dim(padded, 0, axis_count, axis=axis_dim)
    above_part = lax.slice_in_dim(padded, 2, axis_count + 2, axis=axis_dim)
    return jnp.sqrt(degree + 1.0) * above_part + jnp.sqrt(degree) * below_part


def degree_flux(phase_field, axis_dim):
    widths = [(0, 0)] * phase_field.ndim
    widths[axis_dim] = (1, 1)
    return flux_from_padded(jnp.pad(phase_field, widths), axis_dim, 0)


def rusanov(phase_field, up_field, down_field, up_flux, down_flux, speed_bound):
    return 0.5 * (up_flux - down_flux) - 0.5 * speed_bound * (
        up_field - 2.0 * phase_field + down_field
    )


def periodic_term(phase_field, axis_deg, axis_cell, speed_bound):
    flux_dir = degree_flux(phase_field, axis_deg)
    return rusanov(
        phase_field,
        jnp.roll(phase_field, -1, axis_cell),
        jnp.roll(phase_field, 1, axis_cell),
        jnp.roll(flux_dir, -1, axis_cell),
        jnp.roll(flux_dir, 1, axis_cell),
        speed_bound,
    )


def collide_body(k_ref, r_ref, l_ref, o_ref):
    rows, depth, width = k_ref.shape
    chunk = ROW_CHUNK

    def body(step, carry):
        first = step * chunk
        block = k_ref[pl.ds(first, chunk)].reshape(chunk * depth, width)
        z = jnp.dot(block, r_ref[...], preferred_element_type=jnp.float32)
        for i in range(chunk):
            part = z[i * depth : (i + 1) * depth] * l_ref[...]
            o_ref[pl.ds(first + i, 1), :] = jnp.sum(part, axis=0, keepdims=True)
        return carry

    lax.fori_loop(0, rows // chunk, body, 0)


def collide_call(kcat, rhs, lmat):
    return pl.pallas_call(
        collide_body,
        out_shape=jax.ShapeDtypeStruct((kcat.shape[0], rhs.shape[1]), jnp.float32),
        interpret=INTERPRET,
    )(kcat, rhs, lmat)


def shift_permutes(values, axis, holders, count, toward):
    received = []
    for shift in range(1, count):
        if toward:
            pairs = [((h - shift) % count, h) for h in holders]
        else:
            pairs = [(h, (h + shift) % count) for h in holders]
        received.append((shift, lax.ppermute(values, axis, pairs)))
    return received


def per_device(distribution, kernel, pair_kind, low_map, thermal_speed, relax_rate):
    own_count, mode_count, row_count, plane_cells = distribution.shape
    per_vx = mode_count // (NVY * NVZ)
    mode_devs = lax.axis_size("mode")
    species_devs = lax.axis_size("species")
    space_devs = lax.axis_size("space")
    mode_id = lax.axis_index("mode")
    first_vx = mode_id * per_vx
    low_count = low_map.shape[0]
    out_rows = kernel.shape[1]
    species_all = own_count * species_devs

    phase_field = distribution.reshape(own_count, per_vx, NVY, NVZ, row_count, NZ, NY)
    below = lax.ppermute(
        phase_field[:, per_vx - 1 :], "mode", [(i, i + 1) for i in range(mode_devs - 1)]
    )
    above = lax.ppermute(phase_field[:, :1], "mode", [(i + 1, i) for i in range(mode_devs - 1)])
    flux_x = flux_from_padded(jnp.concatenate([below, phase_field, above], axis=1), 1, first_vx)
    up_part = 0.5 * flux_x - 0.5 * bound_x * phase_field
    down_part = -0.5 * flux_x - 0.5 * bound_x * phase_field
    from_next = lax.ppermute(
        up_part[:, :, :, :, :1], "space", [(i + 1, i) for i in range(space_devs - 1)]
    )
    from_prev = lax.ppermute(
        down_part[:, :, :, :, row_count - 1 :], "space", [(i, i + 1) for i in range(space_devs - 1)]
    )
    up_all = jnp.concatenate([up_part[:, :, :, :, 1:], from_next], axis=4)
    down_all = jnp.concatenate([from_prev, down_part[:, :, :, :, : row_count - 1]], axis=4)
    x_term = up_all + down_all + bound_x * phase_field
    y_term = periodic_term(phase_field, 2, 6, bound_y)
    z_term = periodic_term(phase_field, 3, 5, bound_z)
    stream = x_term + y_term + z_term
    advected = phase_field - nu_step * thermal_speed.reshape(own_count, 1, 1, 1, 1, 1, 1) * stream

    cell_count = row_count * plane_cells
    block_cells = cell_count // species_devs
    flat_dist = distribution.reshape(own_count, mode_count, cell_count)
    local_index = low_map - mode_id * mode_count
    owned = (local_index >= 0) & (local_index < mode_count)
    clipped = jnp.clip(local_index, 0, mode_count - 1)
    picked = jnp.where(owned[None, :, None], jnp.take(flat_dist, clipped, axis=1), 0.0).astype(
        jnp.bfloat16
    )
    picked = picked.reshape(own_count, low_count, species_devs, block_cells)
    spread = lax.all_to_all(picked, "species", 2, 0, tiled=True)
    holders = [h for h in range(mode_devs) if h * per_vx <= DEG]
    low_all = spread
    for _, got in shift_permutes(spread, "mode", holders, mode_devs, False):
        low_all = low_all + got
    low_all = low_all.reshape(species_all, low_count, block_cells).astype(jnp.float32)

    chooser = jnp.stack([(pair_kind == k).astype(jnp.float32) for k in range(NKIND)])
    partner = jnp.einsum("ksr,rlc->klsc", chooser, low_all, precision=lax.Precision.HIGHEST)
    part_hi = partner.astype(jnp.bfloat16)
    part_lo = (partner - part_hi.astype(jnp.float32)).astype(jnp.bfloat16)
    rhs = jnp.stack([piece for k in range(NKIND) for piece in (part_hi[k], part_lo[k])])
    rhs = jnp.pad(rhs, ((0, 0), (0, PAD - low_count), (0, 0), (0, 0)))
    rhs = rhs.reshape(2 * NKIND * PAD, species_all * block_cells)
    lmat = jnp.pad(jnp.moveaxis(low_all, 1, 0), ((0, PAD - low_count), (0, 0), (0, 0)))
    lmat = lmat.reshape(PAD, species_all * block_cells)
    kpad = jnp.pad(kernel, ((0, 0), (0, 0), (0, PAD - low_count), (0, PAD - low_count)))
    kcat = jnp.concatenate([kpad[k] for k in range(NKIND) for _ in range(2)], axis=-1)
    gained = collide_call(kcat, rhs, lmat)

    gained = gained.reshape(out_rows, species_devs, 1, own_count, block_cells)
    gained = jnp.broadcast_to(
        gained, (out_rows, species_devs, mode_devs, own_count, block_cells)
    ).reshape(out_rows, species_devs * mode_devs, own_count, block_cells)
    gathered = lax.all_to_all(gained, ("species", "mode"), 1, 1, tiled=True)
    gathered = gathered.reshape(out_rows, species_devs, mode_devs, own_count, block_cells)
    all_gained = jnp.transpose(gathered, (2, 0, 3, 1, 4)).reshape(
        mode_devs * out_rows, own_count, cell_count
    )

    local_modes = mode_id * mode_count + jnp.arange(mode_count)
    match = low_map[None, :] == local_modes[:, None]
    inverse = jnp.argmax(match, axis=1)
    coll_low = jnp.moveaxis(jnp.take(all_gained, inverse, axis=0), 0, 1)
    vx_degree = first_vx + jnp.arange(per_vx)
    degree_total = (
        vx_degree[:, None, None] + jnp.arange(NVY)[None, :, None] + jnp.arange(NVZ)[None, None, :]
    ).reshape(1, mode_count, 1)
    collide = jnp.where(
        degree_total > DEG, -relax_rate.reshape(own_count, 1, 1) * flat_dist, coll_low
    )
    return advected.reshape(
        own_count, mode_count, row_count, plane_cells
    ) + dt_step * collide.reshape(own_count, mode_count, row_count, plane_cells)


def solution(mesh):
    in_specs = (
        P("species", "mode", "space", None),
        P(None, "mode", None, None),
        P(),
        P(),
        P("species"),
        P("species"),
    )
    out_specs = P("species", "mode", "space", None)
    return jax.shard_map(
        per_device, mesh=mesh, in_specs=in_specs, out_specs=out_specs, check_vma=False
    )
```

```python
import jax
import jax.numpy as jnp
from jax import lax
from jax.experimental import pallas as pl
from jax.sharding import PartitionSpec as P

NVY = 8
NVZ = 8
DEG = 7
NKIND = 2
NY = 256
NZ = 2
PAD = 128
ROW_CHUNK = 10

nu_step = 0.0625
dt_step = 0.05
bound_x = 6.7
bound_y = 4.2
bound_z = 4.2

INTERPRET = False


def flux_from_padded(padded, axis_dim, first_degree):
    axis_count = padded.shape[axis_dim] - 2
    dims_shape = [1] * padded.ndim
    dims_shape[axis_dim] = axis_count
    degree = (first_degree + jnp.arange(axis_count)).astype(jnp.float32).reshape(dims_shape)
    below_part = lax.slice_in_dim(padded, 0, axis_count, axis=axis_dim)
    above_part = lax.slice_in_dim(padded, 2, axis_count + 2, axis=axis_dim)
    return jnp.sqrt(degree + 1.0) * above_part + jnp.sqrt(degree) * below_part


def degree_flux(phase_field, axis_dim):
    widths = [(0, 0)] * phase_field.ndim
    widths[axis_dim] = (1, 1)
    return flux_from_padded(jnp.pad(phase_field, widths), axis_dim, 0)


def rusanov(phase_field, up_field, down_field, up_flux, down_flux, speed_bound):
    return 0.5 * (up_flux - down_flux) - 0.5 * speed_bound * (
        up_field - 2.0 * phase_field + down_field
    )


def periodic_term(phase_field, axis_deg, axis_cell, speed_bound):
    flux_dir = degree_flux(phase_field, axis_deg)
    return rusanov(
        phase_field,
        jnp.roll(phase_field, -1, axis_cell),
        jnp.roll(phase_field, 1, axis_cell),
        jnp.roll(flux_dir, -1, axis_cell),
        jnp.roll(flux_dir, 1, axis_cell),
        speed_bound,
    )


def collide_body(k_ref, r_ref, l_ref, o_ref):
    rows, depth, width = k_ref.shape
    chunk = ROW_CHUNK

    def body(step, carry):
        first = step * chunk
        block = k_ref[pl.ds(first, chunk)].reshape(chunk * depth, width)
        z = jnp.dot(block, r_ref[...], preferred_element_type=jnp.float32)
        for i in range(chunk):
            part = z[i * depth : (i + 1) * depth] * l_ref[...]
            o_ref[pl.ds(first + i, 1), :] = jnp.sum(part, axis=0, keepdims=True)
        return carry

    lax.fori_loop(0, rows // chunk, body, 0)


def collide_call(kcat, rhs, lmat):
    return pl.pallas_call(
        collide_body,
        out_shape=jax.ShapeDtypeStruct((kcat.shape[0], rhs.shape[1]), jnp.float32),
        interpret=INTERPRET,
    )(kcat, rhs, lmat)


def shift_permutes(values, axis, holders, count, toward):
    received = []
    for shift in range(1, count):
        if toward:
            pairs = [((h - shift) % count, h) for h in holders]
        else:
            pairs = [(h, (h + shift) % count) for h in holders]
        received.append((shift, lax.ppermute(values, axis, pairs)))
    return received


def per_device(distribution, kernel, pair_kind, low_map, thermal_speed, relax_rate):
    own_count, mode_count, row_count, plane_cells = distribution.shape
    per_vx = mode_count // (NVY * NVZ)
    mode_devs = lax.axis_size("mode")
    species_devs = lax.axis_size("species")
    space_devs = lax.axis_size("space")
    mode_id = lax.axis_index("mode")
    first_vx = mode_id * per_vx
    low_count = low_map.shape[0]
    out_rows = kernel.shape[1]
    species_all = own_count * species_devs

    phase_field = distribution.reshape(own_count, per_vx, NVY, NVZ, row_count, NZ, NY)
    below = lax.ppermute(
        phase_field[:, per_vx - 1 :], "mode", [(i, i + 1) for i in range(mode_devs - 1)]
    )
    above = lax.ppermute(phase_field[:, :1], "mode", [(i + 1, i) for i in range(mode_devs - 1)])
    flux_x = flux_from_padded(jnp.concatenate([below, phase_field, above], axis=1), 1, first_vx)
    up_part = 0.5 * flux_x - 0.5 * bound_x * phase_field
    down_part = -0.5 * flux_x - 0.5 * bound_x * phase_field
    from_next = lax.ppermute(
        up_part[:, :, :, :, :1], "space", [(i + 1, i) for i in range(space_devs - 1)]
    )
    from_prev = lax.ppermute(
        down_part[:, :, :, :, row_count - 1 :], "space", [(i, i + 1) for i in range(space_devs - 1)]
    )
    up_all = jnp.concatenate([up_part[:, :, :, :, 1:], from_next], axis=4)
    down_all = jnp.concatenate([from_prev, down_part[:, :, :, :, : row_count - 1]], axis=4)
    x_term = up_all + down_all + bound_x * phase_field
    y_term = periodic_term(phase_field, 2, 6, bound_y)
    z_term = periodic_term(phase_field, 3, 5, bound_z)
    stream = x_term + y_term + z_term
    advected = phase_field - nu_step * thermal_speed.reshape(own_count, 1, 1, 1, 1, 1, 1) * stream

    cell_count = row_count * plane_cells
    block_cells = cell_count // species_devs
    flat_dist = distribution.reshape(own_count, mode_count, cell_count)
    local_index = low_map - mode_id * mode_count
    owned = (local_index >= 0) & (local_index < mode_count)
    clipped = jnp.clip(local_index, 0, mode_count - 1)
    picked = jnp.where(owned[None, :, None], jnp.take(flat_dist, clipped, axis=1), 0.0).astype(
        jnp.bfloat16
    )
    picked = picked.reshape(own_count, low_count, species_devs, block_cells)
    spread = lax.all_to_all(picked, "species", 2, 0, tiled=True)
    holders = [h for h in range(mode_devs) if h * per_vx <= DEG]
    low_all = spread
    for _, got in shift_permutes(spread, "mode", holders, mode_devs, False):
        low_all = low_all + got
    low_all = low_all.reshape(species_all, low_count, block_cells).astype(jnp.float32)

    chooser = jnp.stack([(pair_kind == k).astype(jnp.float32) for k in range(NKIND)])
    partner = jnp.einsum("ksr,rlc->klsc", chooser, low_all, precision=lax.Precision.HIGHEST)
    part_hi = partner.astype(jnp.bfloat16)
    part_lo = (partner - part_hi.astype(jnp.float32)).astype(jnp.bfloat16)
    rhs = jnp.stack([piece for k in range(NKIND) for piece in (part_hi[k], part_lo[k])])
    rhs = jnp.pad(rhs, ((0, 0), (0, PAD - low_count), (0, 0), (0, 0)))
    rhs = rhs.reshape(2 * NKIND * PAD, species_all * block_cells)
    lmat = jnp.pad(jnp.moveaxis(low_all, 1, 0), ((0, PAD - low_count), (0, 0), (0, 0)))
    lmat = lmat.reshape(PAD, species_all * block_cells)
    kpad = jnp.pad(kernel, ((0, 0), (0, 0), (0, PAD - low_count), (0, PAD - low_count)))
    kcat = jnp.concatenate([kpad[k] for k in range(NKIND) for _ in range(2)], axis=-1)
    gained = collide_call(kcat, rhs, lmat)

    gained = gained.reshape(out_rows, species_devs, 1, own_count, block_cells)
    gained = jnp.broadcast_to(
        gained, (out_rows, species_devs, mode_devs, own_count, block_cells)
    ).reshape(out_rows, species_devs * mode_devs, own_count, block_cells)
    gathered = lax.all_to_all(gained.astype(jnp.bfloat16), ("species", "mode"), 1, 1, tiled=True)
    gathered = gathered.astype(jnp.float32)
    gathered = gathered.reshape(out_rows, species_devs, mode_devs, own_count, block_cells)
    all_gained = jnp.transpose(gathered, (2, 0, 3, 1, 4)).reshape(
        mode_devs * out_rows, own_count, cell_count
    )

    local_modes = mode_id * mode_count + jnp.arange(mode_count)
    match = low_map[None, :] == local_modes[:, None]
    inverse = jnp.argmax(match, axis=1)
    coll_low = jnp.moveaxis(jnp.take(all_gained, inverse, axis=0), 0, 1)
    vx_degree = first_vx + jnp.arange(per_vx)
    degree_total = (
        vx_degree[:, None, None] + jnp.arange(NVY)[None, :, None] + jnp.arange(NVZ)[None, None, :]
    ).reshape(1, mode_count, 1)
    collide = jnp.where(
        degree_total > DEG, -relax_rate.reshape(own_count, 1, 1) * flat_dist, coll_low
    )
    return advected.reshape(
        own_count, mode_count, row_count, plane_cells
    ) + dt_step * collide.reshape(own_count, mode_count, row_count, plane_cells)


def solution(mesh):
    in_specs = (
        P("species", "mode", "space", None),
        P(None, "mode", None, None),
        P(),
        P(),
        P("species"),
        P("species"),
    )
    out_specs = P("species", "mode", "space", None)
    return jax.shard_map(
        per_device, mesh=mesh, in_specs=in_specs, out_specs=out_specs, check_vma=False
    )
```

```python
import jax
import jax.numpy as jnp
from jax import lax
from jax.experimental import pallas as pl
from jax.sharding import PartitionSpec as P

NVY = 8
NVZ = 8
DEG = 7
NKIND = 2
NY = 256
NZ = 2
PAD = 128
ROW_CHUNK = 10

nu_step = 0.0625
dt_step = 0.05
bound_x = 6.7
bound_y = 4.2
bound_z = 4.2

INTERPRET = False


def flux_from_padded(padded, axis_dim, first_degree):
    axis_count = padded.shape[axis_dim] - 2
    dims_shape = [1] * padded.ndim
    dims_shape[axis_dim] = axis_count
    degree = (first_degree + jnp.arange(axis_count)).astype(jnp.float32).reshape(dims_shape)
    below_part = lax.slice_in_dim(padded, 0, axis_count, axis=axis_dim)
    above_part = lax.slice_in_dim(padded, 2, axis_count + 2, axis=axis_dim)
    return jnp.sqrt(degree + 1.0) * above_part + jnp.sqrt(degree) * below_part


def degree_flux(phase_field, axis_dim):
    widths = [(0, 0)] * phase_field.ndim
    widths[axis_dim] = (1, 1)
    return flux_from_padded(jnp.pad(phase_field, widths), axis_dim, 0)


def rusanov(phase_field, up_field, down_field, up_flux, down_flux, speed_bound):
    return 0.5 * (up_flux - down_flux) - 0.5 * speed_bound * (
        up_field - 2.0 * phase_field + down_field
    )


def periodic_term(phase_field, axis_deg, axis_cell, speed_bound):
    flux_dir = degree_flux(phase_field, axis_deg)
    return rusanov(
        phase_field,
        jnp.roll(phase_field, -1, axis_cell),
        jnp.roll(phase_field, 1, axis_cell),
        jnp.roll(flux_dir, -1, axis_cell),
        jnp.roll(flux_dir, 1, axis_cell),
        speed_bound,
    )


def collide_body(k_ref, r_ref, l_ref, o_ref):
    rows, depth, width = k_ref.shape
    chunk = ROW_CHUNK

    def body(step, carry):
        first = step * chunk
        block = k_ref[pl.ds(first, chunk)].reshape(chunk * depth, width)
        z = jnp.dot(block, r_ref[...], preferred_element_type=jnp.float32)
        for i in range(chunk):
            part = z[i * depth : (i + 1) * depth] * l_ref[...]
            o_ref[pl.ds(first + i, 1), :] = jnp.sum(part, axis=0, keepdims=True)
        return carry

    lax.fori_loop(0, rows // chunk, body, 0)


def collide_call(kcat, rhs, lmat):
    return pl.pallas_call(
        collide_body,
        out_shape=jax.ShapeDtypeStruct((kcat.shape[0], rhs.shape[1]), jnp.float32),
        interpret=INTERPRET,
    )(kcat, rhs, lmat)


def shift_permutes(values, axis, holders, count, toward):
    received = []
    for shift in range(1, count):
        if toward:
            pairs = [((h - shift) % count, h) for h in holders]
        else:
            pairs = [(h, (h + shift) % count) for h in holders]
        received.append((shift, lax.ppermute(values, axis, pairs)))
    return received


def per_device(distribution, kernel, pair_kind, low_map, thermal_speed, relax_rate):
    own_count, mode_count, row_count, plane_cells = distribution.shape
    per_vx = mode_count // (NVY * NVZ)
    mode_devs = lax.axis_size("mode")
    species_devs = lax.axis_size("species")
    space_devs = lax.axis_size("space")
    mode_id = lax.axis_index("mode")
    first_vx = mode_id * per_vx
    low_count = low_map.shape[0]
    out_rows = kernel.shape[1]
    species_all = own_count * species_devs

    phase_field = distribution.reshape(own_count, per_vx, NVY, NVZ, row_count, NZ, NY)
    below = lax.ppermute(
        phase_field[:, per_vx - 1 :], "mode", [(i, i + 1) for i in range(mode_devs - 1)]
    )
    above = lax.ppermute(phase_field[:, :1], "mode", [(i + 1, i) for i in range(mode_devs - 1)])
    flux_x = flux_from_padded(jnp.concatenate([below, phase_field, above], axis=1), 1, first_vx)
    up_part = 0.5 * flux_x - 0.5 * bound_x * phase_field
    down_part = -0.5 * flux_x - 0.5 * bound_x * phase_field
    from_next = lax.ppermute(
        up_part[:, :, :, :, :1], "space", [(i + 1, i) for i in range(space_devs - 1)]
    )
    from_prev = lax.ppermute(
        down_part[:, :, :, :, row_count - 1 :], "space", [(i, i + 1) for i in range(space_devs - 1)]
    )
    up_all = jnp.concatenate([up_part[:, :, :, :, 1:], from_next], axis=4)
    down_all = jnp.concatenate([from_prev, down_part[:, :, :, :, : row_count - 1]], axis=4)
    x_term = up_all + down_all + bound_x * phase_field
    y_term = periodic_term(phase_field, 2, 6, bound_y)
    z_term = periodic_term(phase_field, 3, 5, bound_z)
    stream = x_term + y_term + z_term
    advected = phase_field - nu_step * thermal_speed.reshape(own_count, 1, 1, 1, 1, 1, 1) * stream

    cell_count = row_count * plane_cells
    block_cells = cell_count // species_devs
    flat_dist = distribution.reshape(own_count, mode_count, cell_count)
    local_index = low_map - mode_id * mode_count
    owned = (local_index >= 0) & (local_index < mode_count)
    clipped = jnp.clip(local_index, 0, mode_count - 1)
    picked = jnp.where(owned[None, :, None], jnp.take(flat_dist, clipped, axis=1), 0.0).astype(
        jnp.bfloat16
    )
    picked = picked.reshape(own_count, low_count, species_devs, block_cells)
    spread = lax.all_to_all(picked, "species", 2, 0, tiled=True)
    holders = [h for h in range(mode_devs) if h * per_vx <= DEG]
    low_all = spread
    for _, got in shift_permutes(spread, "mode", holders, mode_devs, False):
        low_all = low_all + got
    low_all = low_all.reshape(species_all, low_count, block_cells).astype(jnp.float32)

    chooser = jnp.stack([(pair_kind == k).astype(jnp.float32) for k in range(NKIND)])
    partner = jnp.einsum("ksr,rlc->klsc", chooser, low_all, precision=lax.Precision.HIGHEST)
    part_hi = partner.astype(jnp.bfloat16)
    part_lo = (partner - part_hi.astype(jnp.float32)).astype(jnp.bfloat16)
    rhs = jnp.stack([piece for k in range(NKIND) for piece in (part_hi[k], part_lo[k])])
    rhs = jnp.pad(rhs, ((0, 0), (0, PAD - low_count), (0, 0), (0, 0)))
    rhs = rhs.reshape(2 * NKIND * PAD, species_all * block_cells)
    lmat = jnp.pad(jnp.moveaxis(low_all, 1, 0), ((0, PAD - low_count), (0, 0), (0, 0)))
    lmat = lmat.reshape(PAD, species_all * block_cells)
    kpad = jnp.pad(kernel, ((0, 0), (0, 0), (0, PAD - low_count), (0, PAD - low_count)))
    kcat = jnp.concatenate([kpad[k] for k in range(NKIND) for _ in range(2)], axis=-1)
    gained = collide_call(kcat, rhs, lmat)

    advected, gained = lax.optimization_barrier((advected, gained))
    gained = gained.reshape(out_rows, species_devs, 1, own_count, block_cells)
    gained = jnp.broadcast_to(
        gained, (out_rows, species_devs, mode_devs, own_count, block_cells)
    ).reshape(out_rows, species_devs * mode_devs, own_count, block_cells)
    gathered = lax.all_to_all(gained.astype(jnp.bfloat16), ("species", "mode"), 1, 1, tiled=True)
    gathered = gathered.astype(jnp.float32)
    gathered = gathered.reshape(out_rows, species_devs, mode_devs, own_count, block_cells)
    all_gained = jnp.transpose(gathered, (2, 0, 3, 1, 4)).reshape(
        mode_devs * out_rows, own_count, cell_count
    )

    local_modes = mode_id * mode_count + jnp.arange(mode_count)
    match = low_map[None, :] == local_modes[:, None]
    inverse = jnp.argmax(match, axis=1)
    coll_low = jnp.moveaxis(jnp.take(all_gained, inverse, axis=0), 0, 1)
    vx_degree = first_vx + jnp.arange(per_vx)
    degree_total = (
        vx_degree[:, None, None] + jnp.arange(NVY)[None, :, None] + jnp.arange(NVZ)[None, None, :]
    ).reshape(1, mode_count, 1)
    collide = jnp.where(
        degree_total > DEG, -relax_rate.reshape(own_count, 1, 1) * flat_dist, coll_low
    )
    return advected.reshape(
        own_count, mode_count, row_count, plane_cells
    ) + dt_step * collide.reshape(own_count, mode_count, row_count, plane_cells)


def solution(mesh):
    in_specs = (
        P("species", "mode", "space", None),
        P(None, "mode", None, None),
        P(),
        P(),
        P("species"),
        P("species"),
    )
    out_specs = P("species", "mode", "space", None)
    return jax.shard_map(
        per_device, mesh=mesh, in_specs=in_specs, out_specs=out_specs, check_vma=False
    )
```

```python
import jax
import jax.numpy as jnp
from jax import lax
from jax.experimental import pallas as pl
from jax.sharding import PartitionSpec as P

NVY = 8
NVZ = 8
DEG = 7
NKIND = 2
NY = 256
NZ = 2
PAD = 128
ROW_CHUNK = 10

nu_step = 0.0625
dt_step = 0.05
bound_x = 6.7
bound_y = 4.2
bound_z = 4.2

INTERPRET = False


def flux_from_padded(padded, axis_dim, first_degree):
    axis_count = padded.shape[axis_dim] - 2
    dims_shape = [1] * padded.ndim
    dims_shape[axis_dim] = axis_count
    degree = (first_degree + jnp.arange(axis_count)).astype(jnp.float32).reshape(dims_shape)
    below_part = lax.slice_in_dim(padded, 0, axis_count, axis=axis_dim)
    above_part = lax.slice_in_dim(padded, 2, axis_count + 2, axis=axis_dim)
    return jnp.sqrt(degree + 1.0) * above_part + jnp.sqrt(degree) * below_part


def degree_flux(phase_field, axis_dim):
    widths = [(0, 0)] * phase_field.ndim
    widths[axis_dim] = (1, 1)
    return flux_from_padded(jnp.pad(phase_field, widths), axis_dim, 0)


def rusanov(phase_field, up_field, down_field, up_flux, down_flux, speed_bound):
    return 0.5 * (up_flux - down_flux) - 0.5 * speed_bound * (
        up_field - 2.0 * phase_field + down_field
    )


def periodic_term(phase_field, axis_deg, axis_cell, speed_bound):
    flux_dir = degree_flux(phase_field, axis_deg)
    return rusanov(
        phase_field,
        jnp.roll(phase_field, -1, axis_cell),
        jnp.roll(phase_field, 1, axis_cell),
        jnp.roll(flux_dir, -1, axis_cell),
        jnp.roll(flux_dir, 1, axis_cell),
        speed_bound,
    )


def collide_body(k_ref, r_ref, l_ref, o_ref):
    rows, depth, width = k_ref.shape
    chunk = ROW_CHUNK

    def body(step, carry):
        first = step * chunk
        block = k_ref[pl.ds(first, chunk)].reshape(chunk * depth, width)
        z = jnp.dot(block, r_ref[...], preferred_element_type=jnp.float32)
        for i in range(chunk):
            part = z[i * depth : (i + 1) * depth] * l_ref[...]
            o_ref[pl.ds(first + i, 1), :] = jnp.sum(part, axis=0, keepdims=True)
        return carry

    lax.fori_loop(0, rows // chunk, body, 0)


def collide_call(kcat, rhs, lmat):
    return pl.pallas_call(
        collide_body,
        out_shape=jax.ShapeDtypeStruct((kcat.shape[0], rhs.shape[1]), jnp.float32),
        interpret=INTERPRET,
    )(kcat, rhs, lmat)


def shift_permutes(values, axis, holders, count, toward):
    received = []
    for shift in range(1, count):
        if toward:
            pairs = [((h - shift) % count, h) for h in holders]
        else:
            pairs = [(h, (h + shift) % count) for h in holders]
        received.append((shift, lax.ppermute(values, axis, pairs)))
    return received


def per_device(distribution, kernel, pair_kind, low_map, thermal_speed, relax_rate):
    own_count, mode_count, row_count, plane_cells = distribution.shape
    per_vx = mode_count // (NVY * NVZ)
    mode_devs = lax.axis_size("mode")
    species_devs = lax.axis_size("species")
    space_devs = lax.axis_size("space")
    mode_id = lax.axis_index("mode")
    first_vx = mode_id * per_vx
    low_count = low_map.shape[0]
    out_rows = kernel.shape[1]
    species_all = own_count * species_devs

    phase_field = distribution.reshape(own_count, per_vx, NVY, NVZ, row_count, NZ, NY)
    below = lax.ppermute(
        phase_field[:, per_vx - 1 :], "mode", [(i, i + 1) for i in range(mode_devs - 1)]
    )
    above = lax.ppermute(phase_field[:, :1], "mode", [(i + 1, i) for i in range(mode_devs - 1)])
    flux_x = flux_from_padded(jnp.concatenate([below, phase_field, above], axis=1), 1, first_vx)
    up_part = 0.5 * flux_x - 0.5 * bound_x * phase_field
    down_part = -0.5 * flux_x - 0.5 * bound_x * phase_field
    from_next = lax.ppermute(
        up_part[:, :, :, :, :1], "space", [(i + 1, i) for i in range(space_devs - 1)]
    )
    from_prev = lax.ppermute(
        down_part[:, :, :, :, row_count - 1 :], "space", [(i, i + 1) for i in range(space_devs - 1)]
    )
    up_all = jnp.concatenate([up_part[:, :, :, :, 1:], from_next], axis=4)
    down_all = jnp.concatenate([from_prev, down_part[:, :, :, :, : row_count - 1]], axis=4)
    x_term = up_all + down_all + bound_x * phase_field
    y_term = periodic_term(phase_field, 2, 6, bound_y)
    z_term = periodic_term(phase_field, 3, 5, bound_z)
    stream = x_term + y_term + z_term
    advected = phase_field - nu_step * thermal_speed.reshape(own_count, 1, 1, 1, 1, 1, 1) * stream

    cell_count = row_count * plane_cells
    block_cells = cell_count // species_devs
    flat_dist = distribution.reshape(own_count, mode_count, cell_count)
    local_index = low_map - mode_id * mode_count
    owned = (local_index >= 0) & (local_index < mode_count)
    clipped = jnp.clip(local_index, 0, mode_count - 1)
    picked = jnp.where(owned[None, :, None], jnp.take(flat_dist, clipped, axis=1), 0.0).astype(
        jnp.bfloat16
    )
    picked = picked.reshape(own_count, low_count, species_devs, 1, block_cells)
    picked = jnp.broadcast_to(
        picked, (own_count, low_count, species_devs, mode_devs, block_cells)
    ).reshape(own_count, low_count, species_devs * mode_devs, block_cells)
    spread = lax.all_to_all(picked, ("species", "mode"), 2, 2, tiled=True)
    spread = spread.reshape(own_count, low_count, species_devs, mode_devs, block_cells)
    spread = jnp.sum(spread.astype(jnp.float32), axis=3)
    low_all = jnp.transpose(spread, (2, 0, 1, 3)).reshape(species_all, low_count, block_cells)

    chooser = jnp.stack([(pair_kind == k).astype(jnp.float32) for k in range(NKIND)])
    partner = jnp.einsum("ksr,rlc->klsc", chooser, low_all, precision=lax.Precision.HIGHEST)
    part_hi = partner.astype(jnp.bfloat16)
    part_lo = (partner - part_hi.astype(jnp.float32)).astype(jnp.bfloat16)
    rhs = jnp.stack([piece for k in range(NKIND) for piece in (part_hi[k], part_lo[k])])
    rhs = jnp.pad(rhs, ((0, 0), (0, PAD - low_count), (0, 0), (0, 0)))
    rhs = rhs.reshape(2 * NKIND * PAD, species_all * block_cells)
    lmat = jnp.pad(jnp.moveaxis(low_all, 1, 0), ((0, PAD - low_count), (0, 0), (0, 0)))
    lmat = lmat.reshape(PAD, species_all * block_cells)
    kpad = jnp.pad(kernel, ((0, 0), (0, 0), (0, PAD - low_count), (0, PAD - low_count)))
    kcat = jnp.concatenate([kpad[k] for k in range(NKIND) for _ in range(2)], axis=-1)
    gained = collide_call(kcat, rhs, lmat)

    gained = gained.reshape(out_rows, species_devs, 1, own_count, block_cells)
    gained = jnp.broadcast_to(
        gained, (out_rows, species_devs, mode_devs, own_count, block_cells)
    ).reshape(out_rows, species_devs * mode_devs, own_count, block_cells)
    gathered = lax.all_to_all(gained.astype(jnp.bfloat16), ("species", "mode"), 1, 1, tiled=True)
    gathered = gathered.astype(jnp.float32)
    gathered = gathered.reshape(out_rows, species_devs, mode_devs, own_count, block_cells)
    all_gained = jnp.transpose(gathered, (2, 0, 3, 1, 4)).reshape(
        mode_devs * out_rows, own_count, cell_count
    )

    local_modes = mode_id * mode_count + jnp.arange(mode_count)
    match = low_map[None, :] == local_modes[:, None]
    inverse = jnp.argmax(match, axis=1)
    coll_low = jnp.moveaxis(jnp.take(all_gained, inverse, axis=0), 0, 1)
    vx_degree = first_vx + jnp.arange(per_vx)
    degree_total = (
        vx_degree[:, None, None] + jnp.arange(NVY)[None, :, None] + jnp.arange(NVZ)[None, None, :]
    ).reshape(1, mode_count, 1)
    collide = jnp.where(
        degree_total > DEG, -relax_rate.reshape(own_count, 1, 1) * flat_dist, coll_low
    )
    return advected.reshape(
        own_count, mode_count, row_count, plane_cells
    ) + dt_step * collide.reshape(own_count, mode_count, row_count, plane_cells)


def solution(mesh):
    in_specs = (
        P("species", "mode", "space", None),
        P(None, "mode", None, None),
        P(),
        P(),
        P("species"),
        P("species"),
    )
    out_specs = P("species", "mode", "space", None)
    return jax.shard_map(
        per_device, mesh=mesh, in_specs=in_specs, out_specs=out_specs, check_vma=False
    )
```

```python
import jax
import jax.numpy as jnp
from jax import lax
from jax.experimental import pallas as pl
from jax.sharding import PartitionSpec as P

NVY = 8
NVZ = 8
DEG = 7
NKIND = 2
NY = 256
NZ = 2
PAD = 128
ROW_CHUNK = 10

nu_step = 0.0625
dt_step = 0.05
bound_x = 6.7
bound_y = 4.2
bound_z = 4.2

INTERPRET = False


def flux_from_padded(padded, axis_dim, first_degree):
    axis_count = padded.shape[axis_dim] - 2
    dims_shape = [1] * padded.ndim
    dims_shape[axis_dim] = axis_count
    degree = (first_degree + jnp.arange(axis_count)).astype(jnp.float32).reshape(dims_shape)
    below_part = lax.slice_in_dim(padded, 0, axis_count, axis=axis_dim)
    above_part = lax.slice_in_dim(padded, 2, axis_count + 2, axis=axis_dim)
    return jnp.sqrt(degree + 1.0) * above_part + jnp.sqrt(degree) * below_part


def degree_flux(phase_field, axis_dim):
    widths = [(0, 0)] * phase_field.ndim
    widths[axis_dim] = (1, 1)
    return flux_from_padded(jnp.pad(phase_field, widths), axis_dim, 0)


def rusanov(phase_field, up_field, down_field, up_flux, down_flux, speed_bound):
    return 0.5 * (up_flux - down_flux) - 0.5 * speed_bound * (
        up_field - 2.0 * phase_field + down_field
    )


def periodic_term(phase_field, axis_deg, axis_cell, speed_bound):
    flux_dir = degree_flux(phase_field, axis_deg)
    return rusanov(
        phase_field,
        jnp.roll(phase_field, -1, axis_cell),
        jnp.roll(phase_field, 1, axis_cell),
        jnp.roll(flux_dir, -1, axis_cell),
        jnp.roll(flux_dir, 1, axis_cell),
        speed_bound,
    )


def collide_body(k_ref, r_ref, l_ref, o_ref):
    rows, depth, width = k_ref.shape
    chunk = ROW_CHUNK

    def body(step, carry):
        first = step * chunk
        block = k_ref[pl.ds(first, chunk)].reshape(chunk * depth, width)
        z = jnp.dot(block, r_ref[...], preferred_element_type=jnp.float32)
        for i in range(chunk):
            part = z[i * depth : (i + 1) * depth] * l_ref[...]
            o_ref[pl.ds(first + i, 1), :] = jnp.sum(part, axis=0, keepdims=True)
        return carry

    lax.fori_loop(0, rows // chunk, body, 0)


def collide_call(kcat, rhs, lmat):
    return pl.pallas_call(
        collide_body,
        out_shape=jax.ShapeDtypeStruct((kcat.shape[0], rhs.shape[1]), jnp.float32),
        interpret=INTERPRET,
    )(kcat, rhs, lmat)


def shift_permutes(values, axis, holders, count, toward):
    received = []
    for shift in range(1, count):
        if toward:
            pairs = [((h - shift) % count, h) for h in holders]
        else:
            pairs = [(h, (h + shift) % count) for h in holders]
        received.append((shift, lax.ppermute(values, axis, pairs)))
    return received


def per_device(distribution, kernel, pair_kind, low_map, thermal_speed, relax_rate):
    own_count, mode_count, row_count, plane_cells = distribution.shape
    per_vx = mode_count // (NVY * NVZ)
    mode_devs = lax.axis_size("mode")
    species_devs = lax.axis_size("species")
    space_devs = lax.axis_size("space")
    mode_id = lax.axis_index("mode")
    first_vx = mode_id * per_vx
    low_count = low_map.shape[0]
    out_rows = kernel.shape[1]
    species_all = own_count * species_devs

    phase_field = distribution.reshape(own_count, per_vx, NVY, NVZ, row_count, NZ, NY)
    below = lax.ppermute(
        phase_field[:, per_vx - 1 :], "mode", [(i, i + 1) for i in range(mode_devs - 1)]
    )
    above = lax.ppermute(phase_field[:, :1], "mode", [(i + 1, i) for i in range(mode_devs - 1)])
    flux_x = flux_from_padded(jnp.concatenate([below, phase_field, above], axis=1), 1, first_vx)
    up_part = 0.5 * flux_x - 0.5 * bound_x * phase_field
    down_part = -0.5 * flux_x - 0.5 * bound_x * phase_field
    from_next = lax.ppermute(
        up_part[:, :, :, :, :1], "space", [(i + 1, i) for i in range(space_devs - 1)]
    )
    from_prev = lax.ppermute(
        down_part[:, :, :, :, row_count - 1 :], "space", [(i, i + 1) for i in range(space_devs - 1)]
    )
    up_all = jnp.concatenate([up_part[:, :, :, :, 1:], from_next], axis=4)
    down_all = jnp.concatenate([from_prev, down_part[:, :, :, :, : row_count - 1]], axis=4)
    x_term = up_all + down_all + bound_x * phase_field
    y_term = periodic_term(phase_field, 2, 6, bound_y)
    z_term = periodic_term(phase_field, 3, 5, bound_z)
    stream = x_term + y_term + z_term
    advected = phase_field - nu_step * thermal_speed.reshape(own_count, 1, 1, 1, 1, 1, 1) * stream

    cell_count = row_count * plane_cells
    block_cells = cell_count // species_devs
    flat_dist = distribution.reshape(own_count, mode_count, cell_count)
    local_index = low_map - mode_id * mode_count
    owned = (local_index >= 0) & (local_index < mode_count)
    clipped = jnp.clip(local_index, 0, mode_count - 1)
    picked = jnp.where(owned[None, :, None], jnp.take(flat_dist, clipped, axis=1), 0.0).astype(
        jnp.bfloat16
    )
    picked = picked.reshape(own_count, low_count, species_devs, block_cells)
    spread = lax.all_to_all(picked, "species", 2, 0, tiled=True)
    holders = [h for h in range(mode_devs) if h * per_vx <= DEG]
    low_all = spread
    for _, got in shift_permutes(spread, "mode", holders, mode_devs, False):
        low_all = low_all + got
    low_all = low_all.reshape(species_all, low_count, block_cells).astype(jnp.float32)

    chooser = jnp.stack([(pair_kind == k).astype(jnp.float32) for k in range(NKIND)])
    partner = jnp.einsum("ksr,rlc->klsc", chooser, low_all, precision=lax.Precision.HIGHEST)
    rhs = jnp.pad(partner.astype(jnp.bfloat16), ((0, 0), (0, PAD - low_count), (0, 0), (0, 0)))
    rhs = rhs.reshape(NKIND * PAD, species_all * block_cells)
    lmat = jnp.pad(jnp.moveaxis(low_all, 1, 0), ((0, PAD - low_count), (0, 0), (0, 0)))
    lmat = lmat.reshape(PAD, species_all * block_cells)
    kpad = jnp.pad(kernel, ((0, 0), (0, 0), (0, PAD - low_count), (0, PAD - low_count)))
    kcat = jnp.concatenate([kpad[k] for k in range(NKIND)], axis=-1)
    gained = collide_call(kcat, rhs, lmat)

    gained = gained.reshape(out_rows, species_devs, 1, own_count, block_cells)
    gained = jnp.broadcast_to(
        gained, (out_rows, species_devs, mode_devs, own_count, block_cells)
    ).reshape(out_rows, species_devs * mode_devs, own_count, block_cells)
    gathered = lax.all_to_all(gained.astype(jnp.bfloat16), ("species", "mode"), 1, 1, tiled=True)
    gathered = gathered.astype(jnp.float32)
    gathered = gathered.reshape(out_rows, species_devs, mode_devs, own_count, block_cells)
    all_gained = jnp.transpose(gathered, (2, 0, 3, 1, 4)).reshape(
        mode_devs * out_rows, own_count, cell_count
    )

    local_modes = mode_id * mode_count + jnp.arange(mode_count)
    match = low_map[None, :] == local_modes[:, None]
    inverse = jnp.argmax(match, axis=1)
    coll_low = jnp.moveaxis(jnp.take(all_gained, inverse, axis=0), 0, 1)
    vx_degree = first_vx + jnp.arange(per_vx)
    degree_total = (
        vx_degree[:, None, None] + jnp.arange(NVY)[None, :, None] + jnp.arange(NVZ)[None, None, :]
    ).reshape(1, mode_count, 1)
    collide = jnp.where(
        degree_total > DEG, -relax_rate.reshape(own_count, 1, 1) * flat_dist, coll_low
    )
    return advected.reshape(
        own_count, mode_count, row_count, plane_cells
    ) + dt_step * collide.reshape(own_count, mode_count, row_count, plane_cells)


def solution(mesh):
    in_specs = (
        P("species", "mode", "space", None),
        P(None, "mode", None, None),
        P(),
        P(),
        P("species"),
        P("species"),
    )
    out_specs = P("species", "mode", "space", None)
    return jax.shard_map(
        per_device, mesh=mesh, in_specs=in_specs, out_specs=out_specs, check_vma=False
    )
```

```python
import jax
import jax.numpy as jnp
from jax import lax
from jax.experimental import pallas as pl
from jax.experimental.pallas import tpu as pltpu
from jax.sharding import PartitionSpec as P

NVY = 8
NVZ = 8
DEG = 7
NKIND = 2
NY = 256
NZ = 2
PAD = 128
ROW_CHUNK = 10

nu_step = 0.0625
dt_step = 0.05
bound_x = 6.7
bound_y = 4.2
bound_z = 4.2

INTERPRET = False


def flux_from_padded(padded, axis_dim, first_degree):
    axis_count = padded.shape[axis_dim] - 2
    dims_shape = [1] * padded.ndim
    dims_shape[axis_dim] = axis_count
    degree = (first_degree + jnp.arange(axis_count)).astype(jnp.float32).reshape(dims_shape)
    below_part = lax.slice_in_dim(padded, 0, axis_count, axis=axis_dim)
    above_part = lax.slice_in_dim(padded, 2, axis_count + 2, axis=axis_dim)
    return jnp.sqrt(degree + 1.0) * above_part + jnp.sqrt(degree) * below_part


def degree_flux(phase_field, axis_dim):
    widths = [(0, 0)] * phase_field.ndim
    widths[axis_dim] = (1, 1)
    return flux_from_padded(jnp.pad(phase_field, widths), axis_dim, 0)


def rusanov(phase_field, up_field, down_field, up_flux, down_flux, speed_bound):
    return 0.5 * (up_flux - down_flux) - 0.5 * speed_bound * (
        up_field - 2.0 * phase_field + down_field
    )


def periodic_term(phase_field, axis_deg, axis_cell, speed_bound):
    flux_dir = degree_flux(phase_field, axis_deg)
    return rusanov(
        phase_field,
        jnp.roll(phase_field, -1, axis_cell),
        jnp.roll(phase_field, 1, axis_cell),
        jnp.roll(flux_dir, -1, axis_cell),
        jnp.roll(flux_dir, 1, axis_cell),
        speed_bound,
    )


def collide_body(k_ref, r_ref, l_ref, o_ref):
    rows, depth, width = k_ref.shape
    chunk = ROW_CHUNK

    def body(step, carry):
        first = step * chunk
        block = k_ref[pl.ds(first, chunk)].reshape(chunk * depth, width)
        z = jnp.dot(block, r_ref[...], preferred_element_type=jnp.float32)
        for i in range(chunk):
            part = z[i * depth : (i + 1) * depth] * l_ref[...]
            o_ref[pl.ds(first + i, 1), :] = jnp.sum(part, axis=0, keepdims=True)
        return carry

    lax.fori_loop(0, rows // chunk, body, 0)


def collide_call(kcat, rhs, lmat):
    return pl.pallas_call(
        collide_body,
        out_shape=jax.ShapeDtypeStruct((kcat.shape[0], rhs.shape[1]), jnp.float32),
        interpret=INTERPRET,
    )(kcat, rhs, lmat)


def stream_body(speed_ref, phi_ref, next_ref, prev_ref, o_ref):
    rows, cells = phi_ref.shape[1], phi_ref.shape[2]
    row = lax.broadcasted_iota(jnp.int32, (rows, cells), 0)
    lane = lax.broadcasted_iota(jnp.int32, (rows, cells), 1)
    deg_b = ((row // NVZ) % NVY).astype(jnp.float32)
    deg_c = (row % NVZ).astype(jnp.float32)
    ypos = lane % NY

    def y_up(v):
        return jnp.where(ypos == NY - 1, pltpu.roll(v, NY - 1, 1), pltpu.roll(v, cells - 1, 1))

    def y_down(v):
        return jnp.where(ypos == 0, pltpu.roll(v, cells - NY + 1, 1), pltpu.roll(v, 1, 1))

    def z_up(v):
        return pltpu.roll(v, cells - NY, 1)

    def z_down(v):
        return pltpu.roll(v, NY, 1)

    for s in range(phi_ref.shape[0]):
        x = phi_ref[s]
        flux_y = jnp.sqrt(deg_b + 1.0) * jnp.where(
            deg_b < NVY - 1, pltpu.roll(x, rows - NVZ, 0), 0.0
        ) + jnp.sqrt(deg_b) * jnp.where(deg_b > 0, pltpu.roll(x, NVZ, 0), 0.0)
        flux_z = jnp.sqrt(deg_c + 1.0) * jnp.where(
            deg_c < NVZ - 1, pltpu.roll(x, rows - 1, 0), 0.0
        ) + jnp.sqrt(deg_c) * jnp.where(deg_c > 0, pltpu.roll(x, 1, 0), 0.0)
        y_term = 0.5 * (y_up(flux_y) - y_down(flux_y)) - 0.5 * bound_y * (
            y_up(x) - 2.0 * x + y_down(x)
        )
        z_term = 0.5 * (z_up(flux_z) - z_down(flux_z)) - 0.5 * bound_z * (
            z_up(x) - 2.0 * x + z_down(x)
        )
        x_term = next_ref[s] + prev_ref[s] + bound_x * x
        o_ref[s] = x - nu_step * speed_ref[s] * (x_term + y_term + z_term)


def stream_call(speed, phi, from_next, from_prev):
    vmem = pl.BlockSpec(memory_space=pltpu.VMEM)
    return pl.pallas_call(
        stream_body,
        out_shape=jax.ShapeDtypeStruct(phi.shape, jnp.float32),
        in_specs=[pl.BlockSpec(memory_space=pltpu.SMEM), vmem, vmem, vmem],
        out_specs=vmem,
        interpret=INTERPRET,
    )(speed, phi, from_next, from_prev)


def shift_permutes(values, axis, holders, count, toward):
    received = []
    for shift in range(1, count):
        if toward:
            pairs = [((h - shift) % count, h) for h in holders]
        else:
            pairs = [(h, (h + shift) % count) for h in holders]
        received.append((shift, lax.ppermute(values, axis, pairs)))
    return received


def per_device(distribution, kernel, pair_kind, low_map, thermal_speed, relax_rate):
    own_count, mode_count, row_count, plane_cells = distribution.shape
    per_vx = mode_count // (NVY * NVZ)
    mode_devs = lax.axis_size("mode")
    species_devs = lax.axis_size("species")
    space_devs = lax.axis_size("space")
    mode_id = lax.axis_index("mode")
    first_vx = mode_id * per_vx
    low_count = low_map.shape[0]
    out_rows = kernel.shape[1]
    species_all = own_count * species_devs

    cell_count = row_count * plane_cells
    flat_dist = distribution.reshape(own_count, mode_count, cell_count)
    plane = NVY * NVZ
    below = lax.ppermute(
        flat_dist[:, mode_count - plane :], "mode", [(i, i + 1) for i in range(mode_devs - 1)]
    )
    above = lax.ppermute(flat_dist[:, :plane], "mode", [(i + 1, i) for i in range(mode_devs - 1)])
    padded = jnp.concatenate([below, flat_dist, above], axis=1)
    degree_a = (first_vx + jnp.arange(mode_count) // plane).astype(jnp.float32).reshape(1, -1, 1)
    flux_x = (
        jnp.sqrt(degree_a + 1.0) * padded[:, 2 * plane :]
        + jnp.sqrt(degree_a) * padded[:, : mode_count]
    )
    up_part = 0.5 * flux_x - 0.5 * bound_x * flat_dist
    down_part = -0.5 * flux_x - 0.5 * bound_x * flat_dist
    from_next = lax.ppermute(up_part, "space", [(i + 1, i) for i in range(space_devs - 1)])
    from_prev = lax.ppermute(down_part, "space", [(i, i + 1) for i in range(space_devs - 1)])
    advected = stream_call(thermal_speed, flat_dist, from_next, from_prev)

    block_cells = cell_count // species_devs
    local_index = low_map - mode_id * mode_count
    owned = (local_index >= 0) & (local_index < mode_count)
    clipped = jnp.clip(local_index, 0, mode_count - 1)
    picked = jnp.where(owned[None, :, None], jnp.take(flat_dist, clipped, axis=1), 0.0).astype(
        jnp.bfloat16
    )
    picked = picked.reshape(own_count, low_count, species_devs, block_cells)
    spread = lax.all_to_all(picked, "species", 2, 0, tiled=True)
    holders = [h for h in range(mode_devs) if h * per_vx <= DEG]
    low_all = spread
    for _, got in shift_permutes(spread, "mode", holders, mode_devs, False):
        low_all = low_all + got
    low_all = low_all.reshape(species_all, low_count, block_cells).astype(jnp.float32)

    chooser = jnp.stack([(pair_kind == k).astype(jnp.float32) for k in range(NKIND)])
    partner = jnp.einsum("ksr,rlc->klsc", chooser, low_all, precision=lax.Precision.HIGHEST)
    part_hi = partner.astype(jnp.bfloat16)
    part_lo = (partner - part_hi.astype(jnp.float32)).astype(jnp.bfloat16)
    rhs = jnp.stack([piece for k in range(NKIND) for piece in (part_hi[k], part_lo[k])])
    rhs = jnp.pad(rhs, ((0, 0), (0, PAD - low_count), (0, 0), (0, 0)))
    rhs = rhs.reshape(2 * NKIND * PAD, species_all * block_cells)
    lmat = jnp.pad(jnp.moveaxis(low_all, 1, 0), ((0, PAD - low_count), (0, 0), (0, 0)))
    lmat = lmat.reshape(PAD, species_all * block_cells)
    kpad = jnp.pad(kernel, ((0, 0), (0, 0), (0, PAD - low_count), (0, PAD - low_count)))
    kcat = jnp.concatenate([kpad[k] for k in range(NKIND) for _ in range(2)], axis=-1)
    gained = collide_call(kcat, rhs, lmat)

    gained = gained.reshape(out_rows, species_devs, 1, own_count, block_cells)
    gained = jnp.broadcast_to(
        gained, (out_rows, species_devs, mode_devs, own_count, block_cells)
    ).reshape(out_rows, species_devs * mode_devs, own_count, block_cells)
    gathered = lax.all_to_all(gained.astype(jnp.bfloat16), ("species", "mode"), 1, 1, tiled=True)
    gathered = gathered.astype(jnp.float32)
    gathered = gathered.reshape(out_rows, species_devs, mode_devs, own_count, block_cells)
    all_gained = jnp.transpose(gathered, (2, 0, 3, 1, 4)).reshape(
        mode_devs * out_rows, own_count, cell_count
    )

    local_modes = mode_id * mode_count + jnp.arange(mode_count)
    match = low_map[None, :] == local_modes[:, None]
    inverse = jnp.argmax(match, axis=1)
    coll_low = jnp.moveaxis(jnp.take(all_gained, inverse, axis=0), 0, 1)
    vx_degree = first_vx + jnp.arange(per_vx)
    degree_total = (
        vx_degree[:, None, None] + jnp.arange(NVY)[None, :, None] + jnp.arange(NVZ)[None, None, :]
    ).reshape(1, mode_count, 1)
    collide = jnp.where(
        degree_total > DEG, -relax_rate.reshape(own_count, 1, 1) * flat_dist, coll_low
    )
    return advected.reshape(
        own_count, mode_count, row_count, plane_cells
    ) + dt_step * collide.reshape(own_count, mode_count, row_count, plane_cells)


def solution(mesh):
    in_specs = (
        P("species", "mode", "space", None),
        P(None, "mode", None, None),
        P(),
        P(),
        P("species"),
        P("species"),
    )
    out_specs = P("species", "mode", "space", None)
    return jax.shard_map(
        per_device, mesh=mesh, in_specs=in_specs, out_specs=out_specs, check_vma=False
    )
```

```python
import jax
import jax.numpy as jnp
from jax import lax
from jax.experimental import pallas as pl
from jax.sharding import PartitionSpec as P

NVY = 8
NVZ = 8
DEG = 7
NKIND = 2
NY = 256
NZ = 2
PAD = 128
ROW_CHUNK = 10

nu_step = 0.0625
dt_step = 0.05
bound_x = 6.7
bound_y = 4.2
bound_z = 4.2

INTERPRET = False


def flux_from_padded(padded, axis_dim, first_degree):
    axis_count = padded.shape[axis_dim] - 2
    dims_shape = [1] * padded.ndim
    dims_shape[axis_dim] = axis_count
    degree = (first_degree + jnp.arange(axis_count)).astype(jnp.float32).reshape(dims_shape)
    below_part = lax.slice_in_dim(padded, 0, axis_count, axis=axis_dim)
    above_part = lax.slice_in_dim(padded, 2, axis_count + 2, axis=axis_dim)
    return jnp.sqrt(degree + 1.0) * above_part + jnp.sqrt(degree) * below_part


def degree_flux(phase_field, axis_dim):
    widths = [(0, 0)] * phase_field.ndim
    widths[axis_dim] = (1, 1)
    return flux_from_padded(jnp.pad(phase_field, widths), axis_dim, 0)


def rusanov(phase_field, up_field, down_field, up_flux, down_flux, speed_bound):
    return 0.5 * (up_flux - down_flux) - 0.5 * speed_bound * (
        up_field - 2.0 * phase_field + down_field
    )


def periodic_term(phase_field, axis_deg, axis_cell, speed_bound):
    flux_dir = degree_flux(phase_field, axis_deg)
    return rusanov(
        phase_field,
        jnp.roll(phase_field, -1, axis_cell),
        jnp.roll(phase_field, 1, axis_cell),
        jnp.roll(flux_dir, -1, axis_cell),
        jnp.roll(flux_dir, 1, axis_cell),
        speed_bound,
    )


def collide_body(k_ref, r_ref, l_ref, o_ref):
    rows, depth, width = k_ref.shape
    chunk = ROW_CHUNK

    def body(step, carry):
        first = step * chunk
        block = k_ref[pl.ds(first, chunk)].reshape(chunk * depth, width)
        z = jnp.dot(block, r_ref[...], preferred_element_type=jnp.float32)
        for i in range(chunk):
            part = z[i * depth : (i + 1) * depth] * l_ref[...]
            o_ref[pl.ds(first + i, 1), :] = jnp.sum(part, axis=0, keepdims=True)
        return carry

    lax.fori_loop(0, rows // chunk, body, 0)


def collide_call(kcat, rhs, lmat):
    return pl.pallas_call(
        collide_body,
        out_shape=jax.ShapeDtypeStruct((kcat.shape[0], rhs.shape[1]), jnp.float32),
        interpret=INTERPRET,
    )(kcat, rhs, lmat)


def shift_permutes(values, axis, holders, count, toward):
    received = []
    for shift in range(1, count):
        if toward:
            pairs = [((h - shift) % count, h) for h in holders]
        else:
            pairs = [(h, (h + shift) % count) for h in holders]
        received.append((shift, lax.ppermute(values, axis, pairs)))
    return received


def per_device(distribution, kernel, pair_kind, low_map, thermal_speed, relax_rate):
    own_count, mode_count, row_count, plane_cells = distribution.shape
    per_vx = mode_count // (NVY * NVZ)
    mode_devs = lax.axis_size("mode")
    species_devs = lax.axis_size("species")
    space_devs = lax.axis_size("space")
    mode_id = lax.axis_index("mode")
    first_vx = mode_id * per_vx
    low_count = low_map.shape[0]
    out_rows = kernel.shape[1]
    species_all = own_count * species_devs

    phase_field = distribution.reshape(own_count, per_vx, NVY, NVZ, row_count, NZ, NY)
    below = lax.ppermute(
        phase_field[:, per_vx - 1 :], "mode", [(i, i + 1) for i in range(mode_devs - 1)]
    )
    above = lax.ppermute(phase_field[:, :1], "mode", [(i + 1, i) for i in range(mode_devs - 1)])
    flux_x = flux_from_padded(jnp.concatenate([below, phase_field, above], axis=1), 1, first_vx)
    up_part = 0.5 * flux_x - 0.5 * bound_x * phase_field
    down_part = -0.5 * flux_x - 0.5 * bound_x * phase_field
    from_next = lax.ppermute(
        up_part[:, :, :, :, :1].astype(jnp.float16),
        "space",
        [(i + 1, i) for i in range(space_devs - 1)],
    ).astype(jnp.float32)
    from_prev = lax.ppermute(
        down_part[:, :, :, :, row_count - 1 :].astype(jnp.float16),
        "space",
        [(i, i + 1) for i in range(space_devs - 1)],
    ).astype(jnp.float32)
    up_all = jnp.concatenate([up_part[:, :, :, :, 1:], from_next], axis=4)
    down_all = jnp.concatenate([from_prev, down_part[:, :, :, :, : row_count - 1]], axis=4)
    x_term = up_all + down_all + bound_x * phase_field
    y_term = periodic_term(phase_field, 2, 6, bound_y)
    z_term = periodic_term(phase_field, 3, 5, bound_z)
    stream = x_term + y_term + z_term
    advected = phase_field - nu_step * thermal_speed.reshape(own_count, 1, 1, 1, 1, 1, 1) * stream

    cell_count = row_count * plane_cells
    block_cells = cell_count // species_devs
    flat_dist = distribution.reshape(own_count, mode_count, cell_count)
    local_index = low_map - mode_id * mode_count
    owned = (local_index >= 0) & (local_index < mode_count)
    clipped = jnp.clip(local_index, 0, mode_count - 1)
    picked = jnp.where(owned[None, :, None], jnp.take(flat_dist, clipped, axis=1), 0.0).astype(
        jnp.bfloat16
    )
    picked = picked.reshape(own_count, low_count, species_devs, block_cells)
    spread = lax.all_to_all(picked, "species", 2, 0, tiled=True)
    holders = [h for h in range(mode_devs) if h * per_vx <= DEG]
    low_all = spread
    for _, got in shift_permutes(spread, "mode", holders, mode_devs, False):
        low_all = low_all + got
    low_all = low_all.reshape(species_all, low_count, block_cells).astype(jnp.float32)

    chooser = jnp.stack([(pair_kind == k).astype(jnp.float32) for k in range(NKIND)])
    partner = jnp.einsum("ksr,rlc->klsc", chooser, low_all, precision=lax.Precision.HIGHEST)
    part_hi = partner.astype(jnp.bfloat16)
    part_lo = (partner - part_hi.astype(jnp.float32)).astype(jnp.bfloat16)
    rhs = jnp.stack([piece for k in range(NKIND) for piece in (part_hi[k], part_lo[k])])
    rhs = jnp.pad(rhs, ((0, 0), (0, PAD - low_count), (0, 0), (0, 0)))
    rhs = rhs.reshape(2 * NKIND * PAD, species_all * block_cells)
    lmat = jnp.pad(jnp.moveaxis(low_all, 1, 0), ((0, PAD - low_count), (0, 0), (0, 0)))
    lmat = lmat.reshape(PAD, species_all * block_cells)
    kpad = jnp.pad(kernel, ((0, 0), (0, 0), (0, PAD - low_count), (0, PAD - low_count)))
    kcat = jnp.concatenate([kpad[k] for k in range(NKIND) for _ in range(2)], axis=-1)
    gained = collide_call(kcat, rhs, lmat)

    gained = gained.reshape(out_rows, species_devs, 1, own_count, block_cells)
    gained = jnp.broadcast_to(
        gained, (out_rows, species_devs, mode_devs, own_count, block_cells)
    ).reshape(out_rows, species_devs * mode_devs, own_count, block_cells)
    gathered = lax.all_to_all(gained.astype(jnp.bfloat16), ("species", "mode"), 1, 1, tiled=True)
    gathered = gathered.astype(jnp.float32)
    gathered = gathered.reshape(out_rows, species_devs, mode_devs, own_count, block_cells)
    all_gained = jnp.transpose(gathered, (2, 0, 3, 1, 4)).reshape(
        mode_devs * out_rows, own_count, cell_count
    )

    local_modes = mode_id * mode_count + jnp.arange(mode_count)
    match = low_map[None, :] == local_modes[:, None]
    inverse = jnp.argmax(match, axis=1)
    coll_low = jnp.moveaxis(jnp.take(all_gained, inverse, axis=0), 0, 1)
    vx_degree = first_vx + jnp.arange(per_vx)
    degree_total = (
        vx_degree[:, None, None] + jnp.arange(NVY)[None, :, None] + jnp.arange(NVZ)[None, None, :]
    ).reshape(1, mode_count, 1)
    collide = jnp.where(
        degree_total > DEG, -relax_rate.reshape(own_count, 1, 1) * flat_dist, coll_low
    )
    return advected.reshape(
        own_count, mode_count, row_count, plane_cells
    ) + dt_step * collide.reshape(own_count, mode_count, row_count, plane_cells)


def solution(mesh):
    in_specs = (
        P("species", "mode", "space", None),
        P(None, "mode", None, None),
        P(),
        P(),
        P("species"),
        P("species"),
    )
    out_specs = P("species", "mode", "space", None)
    return jax.shard_map(
        per_device, mesh=mesh, in_specs=in_specs, out_specs=out_specs, check_vma=False
    )
```

```python
import jax
import jax.numpy as jnp
from jax import lax
from jax.experimental import pallas as pl
from jax.sharding import PartitionSpec as P

NVY = 8
NVZ = 8
DEG = 7
NKIND = 2
NY = 256
NZ = 2
PAD = 128
ROW_CHUNK = 10

nu_step = 0.0625
dt_step = 0.05
bound_x = 6.7
bound_y = 4.2
bound_z = 4.2

INTERPRET = False


def flux_from_padded(padded, axis_dim, first_degree):
    axis_count = padded.shape[axis_dim] - 2
    dims_shape = [1] * padded.ndim
    dims_shape[axis_dim] = axis_count
    degree = (first_degree + jnp.arange(axis_count)).astype(jnp.float32).reshape(dims_shape)
    below_part = lax.slice_in_dim(padded, 0, axis_count, axis=axis_dim)
    above_part = lax.slice_in_dim(padded, 2, axis_count + 2, axis=axis_dim)
    return jnp.sqrt(degree + 1.0) * above_part + jnp.sqrt(degree) * below_part


def degree_flux(phase_field, axis_dim):
    widths = [(0, 0)] * phase_field.ndim
    widths[axis_dim] = (1, 1)
    return flux_from_padded(jnp.pad(phase_field, widths), axis_dim, 0)


def rusanov(phase_field, up_field, down_field, up_flux, down_flux, speed_bound):
    return 0.5 * (up_flux - down_flux) - 0.5 * speed_bound * (
        up_field - 2.0 * phase_field + down_field
    )


def periodic_term(phase_field, axis_deg, axis_cell, speed_bound):
    flux_dir = degree_flux(phase_field, axis_deg)
    return rusanov(
        phase_field,
        jnp.roll(phase_field, -1, axis_cell),
        jnp.roll(phase_field, 1, axis_cell),
        jnp.roll(flux_dir, -1, axis_cell),
        jnp.roll(flux_dir, 1, axis_cell),
        speed_bound,
    )


def collide_body(k_ref, r_ref, l_ref, o_ref):
    rows, depth, width = k_ref.shape
    chunk = ROW_CHUNK

    def body(step, carry):
        first = step * chunk
        block = k_ref[pl.ds(first, chunk)].reshape(chunk * depth, width)
        z = jnp.dot(block, r_ref[...], preferred_element_type=jnp.float32)
        for i in range(chunk):
            part = z[i * depth : (i + 1) * depth] * l_ref[...]
            o_ref[pl.ds(first + i, 1), :] = jnp.sum(part, axis=0, keepdims=True)
        return carry

    lax.fori_loop(0, rows // chunk, body, 0)


def collide_call(kcat, rhs, lmat):
    return pl.pallas_call(
        collide_body,
        out_shape=jax.ShapeDtypeStruct((kcat.shape[0], rhs.shape[1]), jnp.float32),
        interpret=INTERPRET,
    )(kcat, rhs, lmat)


def shift_permutes(values, axis, holders, count, toward):
    received = []
    for shift in range(1, count):
        if toward:
            pairs = [((h - shift) % count, h) for h in holders]
        else:
            pairs = [(h, (h + shift) % count) for h in holders]
        received.append((shift, lax.ppermute(values, axis, pairs)))
    return received


def per_device(distribution, kernel, pair_kind, low_map, thermal_speed, relax_rate):
    own_count, mode_count, row_count, plane_cells = distribution.shape
    per_vx = mode_count // (NVY * NVZ)
    mode_devs = lax.axis_size("mode")
    species_devs = lax.axis_size("species")
    space_devs = lax.axis_size("space")
    mode_id = lax.axis_index("mode")
    first_vx = mode_id * per_vx
    low_count = low_map.shape[0]
    out_rows = kernel.shape[1]
    species_all = own_count * species_devs

    cell_count = row_count * plane_cells
    block_cells = cell_count // species_devs
    flat_dist = distribution.reshape(own_count, mode_count, cell_count)
    local_index = low_map - mode_id * mode_count
    owned = (local_index >= 0) & (local_index < mode_count)
    clipped = jnp.clip(local_index, 0, mode_count - 1)
    picked = jnp.where(owned[None, :, None], jnp.take(flat_dist, clipped, axis=1), 0.0).astype(
        jnp.bfloat16
    )
    picked = picked.reshape(own_count, low_count, species_devs, block_cells)
    picked, distribution = lax.optimization_barrier((picked, distribution))
    spread = lax.all_to_all(picked, "species", 2, 0, tiled=True)
    phase_field = distribution.reshape(own_count, per_vx, NVY, NVZ, row_count, NZ, NY)
    below = lax.ppermute(
        phase_field[:, per_vx - 1 :], "mode", [(i, i + 1) for i in range(mode_devs - 1)]
    )
    above = lax.ppermute(phase_field[:, :1], "mode", [(i + 1, i) for i in range(mode_devs - 1)])
    flux_x = flux_from_padded(jnp.concatenate([below, phase_field, above], axis=1), 1, first_vx)
    up_part = 0.5 * flux_x - 0.5 * bound_x * phase_field
    down_part = -0.5 * flux_x - 0.5 * bound_x * phase_field
    from_next = lax.ppermute(
        up_part[:, :, :, :, :1].astype(jnp.float16),
        "space",
        [(i + 1, i) for i in range(space_devs - 1)],
    ).astype(jnp.float32)
    from_prev = lax.ppermute(
        down_part[:, :, :, :, row_count - 1 :].astype(jnp.float16),
        "space",
        [(i, i + 1) for i in range(space_devs - 1)],
    ).astype(jnp.float32)
    up_all = jnp.concatenate([up_part[:, :, :, :, 1:], from_next], axis=4)
    down_all = jnp.concatenate([from_prev, down_part[:, :, :, :, : row_count - 1]], axis=4)
    x_term = up_all + down_all + bound_x * phase_field
    y_term = periodic_term(phase_field, 2, 6, bound_y)
    z_term = periodic_term(phase_field, 3, 5, bound_z)
    stream = x_term + y_term + z_term
    advected = phase_field - nu_step * thermal_speed.reshape(own_count, 1, 1, 1, 1, 1, 1) * stream

    holders = [h for h in range(mode_devs) if h * per_vx <= DEG]
    low_all = spread
    for _, got in shift_permutes(spread, "mode", holders, mode_devs, False):
        low_all = low_all + got
    low_all = low_all.reshape(species_all, low_count, block_cells).astype(jnp.float32)

    chooser = jnp.stack([(pair_kind == k).astype(jnp.float32) for k in range(NKIND)])
    partner = jnp.einsum("ksr,rlc->klsc", chooser, low_all, precision=lax.Precision.HIGHEST)
    part_hi = partner.astype(jnp.bfloat16)
    part_lo = (partner - part_hi.astype(jnp.float32)).astype(jnp.bfloat16)
    rhs = jnp.stack([piece for k in range(NKIND) for piece in (part_hi[k], part_lo[k])])
    rhs = jnp.pad(rhs, ((0, 0), (0, PAD - low_count), (0, 0), (0, 0)))
    rhs = rhs.reshape(2 * NKIND * PAD, species_all * block_cells)
    lmat = jnp.pad(jnp.moveaxis(low_all, 1, 0), ((0, PAD - low_count), (0, 0), (0, 0)))
    lmat = lmat.reshape(PAD, species_all * block_cells)
    kpad = jnp.pad(kernel, ((0, 0), (0, 0), (0, PAD - low_count), (0, PAD - low_count)))
    kcat = jnp.concatenate([kpad[k] for k in range(NKIND) for _ in range(2)], axis=-1)
    gained = collide_call(kcat, rhs, lmat)

    gained = gained.reshape(out_rows, species_devs, 1, own_count, block_cells)
    gained = jnp.broadcast_to(
        gained, (out_rows, species_devs, mode_devs, own_count, block_cells)
    ).reshape(out_rows, species_devs * mode_devs, own_count, block_cells)
    gathered = lax.all_to_all(gained.astype(jnp.bfloat16), ("species", "mode"), 1, 1, tiled=True)
    gathered = gathered.astype(jnp.float32)
    gathered = gathered.reshape(out_rows, species_devs, mode_devs, own_count, block_cells)
    all_gained = jnp.transpose(gathered, (2, 0, 3, 1, 4)).reshape(
        mode_devs * out_rows, own_count, cell_count
    )

    local_modes = mode_id * mode_count + jnp.arange(mode_count)
    match = low_map[None, :] == local_modes[:, None]
    inverse = jnp.argmax(match, axis=1)
    coll_low = jnp.moveaxis(jnp.take(all_gained, inverse, axis=0), 0, 1)
    vx_degree = first_vx + jnp.arange(per_vx)
    degree_total = (
        vx_degree[:, None, None] + jnp.arange(NVY)[None, :, None] + jnp.arange(NVZ)[None, None, :]
    ).reshape(1, mode_count, 1)
    collide = jnp.where(
        degree_total > DEG, -relax_rate.reshape(own_count, 1, 1) * flat_dist, coll_low
    )
    return advected.reshape(
        own_count, mode_count, row_count, plane_cells
    ) + dt_step * collide.reshape(own_count, mode_count, row_count, plane_cells)


def solution(mesh):
    in_specs = (
        P("species", "mode", "space", None),
        P(None, "mode", None, None),
        P(),
        P(),
        P("species"),
        P("species"),
    )
    out_specs = P("species", "mode", "space", None)
    return jax.shard_map(
        per_device, mesh=mesh, in_specs=in_specs, out_specs=out_specs, check_vma=False
    )
```

```python
import jax
import jax.numpy as jnp
from jax import lax
from jax.experimental import pallas as pl
from jax.sharding import PartitionSpec as P

NVY = 8
NVZ = 8
DEG = 7
NKIND = 2
NY = 256
NZ = 2
PAD = 128
ROW_CHUNK = 10

nu_step = 0.0625
dt_step = 0.05
bound_x = 6.7
bound_y = 4.2
bound_z = 4.2

INTERPRET = False


def flux_from_padded(padded, axis_dim, first_degree):
    axis_count = padded.shape[axis_dim] - 2
    dims_shape = [1] * padded.ndim
    dims_shape[axis_dim] = axis_count
    degree = (first_degree + jnp.arange(axis_count)).astype(jnp.float32).reshape(dims_shape)
    below_part = lax.slice_in_dim(padded, 0, axis_count, axis=axis_dim)
    above_part = lax.slice_in_dim(padded, 2, axis_count + 2, axis=axis_dim)
    return jnp.sqrt(degree + 1.0) * above_part + jnp.sqrt(degree) * below_part


def degree_flux(phase_field, axis_dim):
    widths = [(0, 0)] * phase_field.ndim
    widths[axis_dim] = (1, 1)
    return flux_from_padded(jnp.pad(phase_field, widths), axis_dim, 0)


def rusanov(phase_field, up_field, down_field, up_flux, down_flux, speed_bound):
    return 0.5 * (up_flux - down_flux) - 0.5 * speed_bound * (
        up_field - 2.0 * phase_field + down_field
    )


def periodic_term(phase_field, axis_deg, axis_cell, speed_bound):
    flux_dir = degree_flux(phase_field, axis_deg)
    return rusanov(
        phase_field,
        jnp.roll(phase_field, -1, axis_cell),
        jnp.roll(phase_field, 1, axis_cell),
        jnp.roll(flux_dir, -1, axis_cell),
        jnp.roll(flux_dir, 1, axis_cell),
        speed_bound,
    )


def collide_body(k_ref, r_ref, l_ref, o_ref):
    rows, depth, width = k_ref.shape
    chunk = ROW_CHUNK

    def body(step, carry):
        first = step * chunk
        block = k_ref[pl.ds(first, chunk)].reshape(chunk * depth, width)
        z = jnp.dot(block, r_ref[...], preferred_element_type=jnp.float32)
        for i in range(chunk):
            part = z[i * depth : (i + 1) * depth] * l_ref[...]
            o_ref[pl.ds(first + i, 1), :] = jnp.sum(part, axis=0, keepdims=True)
        return carry

    lax.fori_loop(0, rows // chunk, body, 0)


def collide_call(kcat, rhs, lmat):
    return pl.pallas_call(
        collide_body,
        out_shape=jax.ShapeDtypeStruct((kcat.shape[0], rhs.shape[1]), jnp.float32),
        interpret=INTERPRET,
    )(kcat, rhs, lmat)


def shift_permutes(values, axis, holders, count, toward):
    received = []
    for shift in range(1, count):
        if toward:
            pairs = [((h - shift) % count, h) for h in holders]
        else:
            pairs = [(h, (h + shift) % count) for h in holders]
        received.append((shift, lax.ppermute(values, axis, pairs)))
    return received


def per_device(distribution, kernel, pair_kind, low_map, thermal_speed, relax_rate):
    own_count, mode_count, row_count, plane_cells = distribution.shape
    per_vx = mode_count // (NVY * NVZ)
    mode_devs = lax.axis_size("mode")
    species_devs = lax.axis_size("species")
    space_devs = lax.axis_size("space")
    mode_id = lax.axis_index("mode")
    first_vx = mode_id * per_vx
    low_count = low_map.shape[0]
    out_rows = kernel.shape[1]
    species_all = own_count * species_devs

    phase_field = distribution.reshape(own_count, per_vx, NVY, NVZ, row_count, NZ, NY)
    below = lax.ppermute(
        phase_field[:, per_vx - 1 :].astype(jnp.float16),
        "mode",
        [(i, i + 1) for i in range(mode_devs - 1)],
    ).astype(jnp.float32)
    above = lax.ppermute(
        phase_field[:, :1].astype(jnp.float16), "mode", [(i + 1, i) for i in range(mode_devs - 1)]
    ).astype(jnp.float32)
    flux_x = flux_from_padded(jnp.concatenate([below, phase_field, above], axis=1), 1, first_vx)
    up_part = 0.5 * flux_x - 0.5 * bound_x * phase_field
    down_part = -0.5 * flux_x - 0.5 * bound_x * phase_field
    from_next = lax.ppermute(
        up_part[:, :, :, :, :1].astype(jnp.float16),
        "space",
        [(i + 1, i) for i in range(space_devs - 1)],
    ).astype(jnp.float32)
    from_prev = lax.ppermute(
        down_part[:, :, :, :, row_count - 1 :].astype(jnp.float16),
        "space",
        [(i, i + 1) for i in range(space_devs - 1)],
    ).astype(jnp.float32)
    up_all = jnp.concatenate([up_part[:, :, :, :, 1:], from_next], axis=4)
    down_all = jnp.concatenate([from_prev, down_part[:, :, :, :, : row_count - 1]], axis=4)
    x_term = up_all + down_all + bound_x * phase_field
    y_term = periodic_term(phase_field, 2, 6, bound_y)
    z_term = periodic_term(phase_field, 3, 5, bound_z)
    stream = x_term + y_term + z_term
    advected = phase_field - nu_step * thermal_speed.reshape(own_count, 1, 1, 1, 1, 1, 1) * stream

    cell_count = row_count * plane_cells
    block_cells = cell_count // species_devs
    flat_dist = distribution.reshape(own_count, mode_count, cell_count)
    local_index = low_map - mode_id * mode_count
    owned = (local_index >= 0) & (local_index < mode_count)
    clipped = jnp.clip(local_index, 0, mode_count - 1)
    picked = jnp.where(owned[None, :, None], jnp.take(flat_dist, clipped, axis=1), 0.0).astype(
        jnp.bfloat16
    )
    picked = picked.reshape(own_count, low_count, species_devs, block_cells)
    spread = lax.all_to_all(picked, "species", 2, 0, tiled=True)
    holders = [h for h in range(mode_devs) if h * per_vx <= DEG]
    low_all = spread
    for _, got in shift_permutes(spread, "mode", holders, mode_devs, False):
        low_all = low_all + got
    low_all = low_all.reshape(species_all, low_count, block_cells).astype(jnp.float32)

    chooser = jnp.stack([(pair_kind == k).astype(jnp.float32) for k in range(NKIND)])
    partner = jnp.einsum("ksr,rlc->klsc", chooser, low_all, precision=lax.Precision.HIGHEST)
    part_hi = partner.astype(jnp.bfloat16)
    part_lo = (partner - part_hi.astype(jnp.float32)).astype(jnp.bfloat16)
    rhs = jnp.stack([piece for k in range(NKIND) for piece in (part_hi[k], part_lo[k])])
    rhs = jnp.pad(rhs, ((0, 0), (0, PAD - low_count), (0, 0), (0, 0)))
    rhs = rhs.reshape(2 * NKIND * PAD, species_all * block_cells)
    lmat = jnp.pad(jnp.moveaxis(low_all, 1, 0), ((0, PAD - low_count), (0, 0), (0, 0)))
    lmat = lmat.reshape(PAD, species_all * block_cells)
    kpad = jnp.pad(kernel, ((0, 0), (0, 0), (0, PAD - low_count), (0, PAD - low_count)))
    kcat = jnp.concatenate([kpad[k] for k in range(NKIND) for _ in range(2)], axis=-1)
    gained = collide_call(kcat, rhs, lmat)

    gained = gained.reshape(out_rows, species_devs, 1, own_count, block_cells)
    gained = jnp.broadcast_to(
        gained, (out_rows, species_devs, mode_devs, own_count, block_cells)
    ).reshape(out_rows, species_devs * mode_devs, own_count, block_cells)
    gathered = lax.all_to_all(gained.astype(jnp.bfloat16), ("species", "mode"), 1, 1, tiled=True)
    gathered = gathered.astype(jnp.float32)
    gathered = gathered.reshape(out_rows, species_devs, mode_devs, own_count, block_cells)
    all_gained = jnp.transpose(gathered, (2, 0, 3, 1, 4)).reshape(
        mode_devs * out_rows, own_count, cell_count
    )

    local_modes = mode_id * mode_count + jnp.arange(mode_count)
    match = low_map[None, :] == local_modes[:, None]
    inverse = jnp.argmax(match, axis=1)
    coll_low = jnp.moveaxis(jnp.take(all_gained, inverse, axis=0), 0, 1)
    vx_degree = first_vx + jnp.arange(per_vx)
    degree_total = (
        vx_degree[:, None, None] + jnp.arange(NVY)[None, :, None] + jnp.arange(NVZ)[None, None, :]
    ).reshape(1, mode_count, 1)
    collide = jnp.where(
        degree_total > DEG, -relax_rate.reshape(own_count, 1, 1) * flat_dist, coll_low
    )
    return advected.reshape(
        own_count, mode_count, row_count, plane_cells
    ) + dt_step * collide.reshape(own_count, mode_count, row_count, plane_cells)


def solution(mesh):
    in_specs = (
        P("species", "mode", "space", None),
        P(None, "mode", None, None),
        P(),
        P(),
        P("species"),
        P("species"),
    )
    out_specs = P("species", "mode", "space", None)
    return jax.shard_map(
        per_device, mesh=mesh, in_specs=in_specs, out_specs=out_specs, check_vma=False
    )
```

```python
import jax
import jax.numpy as jnp
from jax import lax
from jax.experimental import pallas as pl
from jax.sharding import PartitionSpec as P

NVY = 8
NVZ = 8
DEG = 7
NKIND = 2
NY = 256
NZ = 2
PAD = 128
ROW_CHUNK = 10

nu_step = 0.0625
dt_step = 0.05
bound_x = 6.7
bound_y = 4.2
bound_z = 4.2

INTERPRET = False


def flux_from_padded(padded, axis_dim, first_degree):
    axis_count = padded.shape[axis_dim] - 2
    dims_shape = [1] * padded.ndim
    dims_shape[axis_dim] = axis_count
    degree = (first_degree + jnp.arange(axis_count)).astype(jnp.float32).reshape(dims_shape)
    below_part = lax.slice_in_dim(padded, 0, axis_count, axis=axis_dim)
    above_part = lax.slice_in_dim(padded, 2, axis_count + 2, axis=axis_dim)
    return jnp.sqrt(degree + 1.0) * above_part + jnp.sqrt(degree) * below_part


def degree_flux(phase_field, axis_dim):
    widths = [(0, 0)] * phase_field.ndim
    widths[axis_dim] = (1, 1)
    return flux_from_padded(jnp.pad(phase_field, widths), axis_dim, 0)


def rusanov(phase_field, up_field, down_field, up_flux, down_flux, speed_bound):
    return 0.5 * (up_flux - down_flux) - 0.5 * speed_bound * (
        up_field - 2.0 * phase_field + down_field
    )


def periodic_term(phase_field, axis_deg, axis_cell, speed_bound):
    flux_dir = degree_flux(phase_field, axis_deg)
    return rusanov(
        phase_field,
        jnp.roll(phase_field, -1, axis_cell),
        jnp.roll(phase_field, 1, axis_cell),
        jnp.roll(flux_dir, -1, axis_cell),
        jnp.roll(flux_dir, 1, axis_cell),
        speed_bound,
    )


def collide_body(k_ref, r_ref, l_ref, o_ref):
    rows, depth, width = k_ref.shape
    chunk = ROW_CHUNK

    def body(step, carry):
        first = step * chunk
        block = k_ref[pl.ds(first, chunk)].reshape(chunk * depth, width)
        z = jnp.dot(block, r_ref[...], preferred_element_type=jnp.float32)
        for i in range(chunk):
            part = z[i * depth : (i + 1) * depth] * l_ref[...]
            o_ref[pl.ds(first + i, 1), :] = jnp.sum(part, axis=0, keepdims=True)
        return carry

    lax.fori_loop(0, rows // chunk, body, 0)


def collide_call(kcat, rhs, lmat):
    return pl.pallas_call(
        collide_body,
        out_shape=jax.ShapeDtypeStruct((kcat.shape[0], rhs.shape[1]), jnp.float32),
        interpret=INTERPRET,
    )(kcat, rhs, lmat)


def shift_permutes(values, axis, holders, count, toward):
    received = []
    for shift in range(1, count):
        if toward:
            pairs = [((h - shift) % count, h) for h in holders]
        else:
            pairs = [(h, (h + shift) % count) for h in holders]
        received.append((shift, lax.ppermute(values, axis, pairs)))
    return received


def per_device(distribution, kernel, pair_kind, low_map, thermal_speed, relax_rate):
    own_count, mode_count, row_count, plane_cells = distribution.shape
    per_vx = mode_count // (NVY * NVZ)
    mode_devs = lax.axis_size("mode")
    species_devs = lax.axis_size("species")
    space_devs = lax.axis_size("space")
    mode_id = lax.axis_index("mode")
    first_vx = mode_id * per_vx
    low_count = low_map.shape[0]
    out_rows = kernel.shape[1]
    species_all = own_count * species_devs

    phase_field = distribution.reshape(own_count, per_vx, NVY, NVZ, row_count, NZ, NY)
    below = lax.ppermute(
        phase_field[:, per_vx - 1 :].astype(jnp.float16),
        "mode",
        [(i, i + 1) for i in range(mode_devs - 1)],
    ).astype(jnp.float32)
    above = lax.ppermute(
        phase_field[:, :1].astype(jnp.float16), "mode", [(i + 1, i) for i in range(mode_devs - 1)]
    ).astype(jnp.float32)
    flux_x = flux_from_padded(jnp.concatenate([below, phase_field, above], axis=1), 1, first_vx)
    up_part = 0.5 * flux_x - 0.5 * bound_x * phase_field
    down_part = -0.5 * flux_x - 0.5 * bound_x * phase_field
    cell_count = row_count * plane_cells
    block_cells = cell_count // species_devs
    flat_dist = distribution.reshape(own_count, mode_count, cell_count)
    local_index = low_map - mode_id * mode_count
    owned = (local_index >= 0) & (local_index < mode_count)
    clipped = jnp.clip(local_index, 0, mode_count - 1)
    picked = jnp.where(owned[None, :, None], jnp.take(flat_dist, clipped, axis=1), 0.0).astype(
        jnp.bfloat16
    )
    picked = picked.reshape(own_count, low_count, species_devs, block_cells)
    spread = lax.all_to_all(picked, "species", 2, 0, tiled=True)
    up_part, down_part, spread = lax.optimization_barrier((up_part, down_part, spread))
    from_next = lax.ppermute(
        up_part[:, :, :, :, :1].astype(jnp.float16),
        "space",
        [(i + 1, i) for i in range(space_devs - 1)],
    ).astype(jnp.float32)
    from_prev = lax.ppermute(
        down_part[:, :, :, :, row_count - 1 :].astype(jnp.float16),
        "space",
        [(i, i + 1) for i in range(space_devs - 1)],
    ).astype(jnp.float32)
    holders = [h for h in range(mode_devs) if h * per_vx <= DEG]
    up_all = jnp.concatenate([up_part[:, :, :, :, 1:], from_next], axis=4)
    down_all = jnp.concatenate([from_prev, down_part[:, :, :, :, : row_count - 1]], axis=4)
    x_term = up_all + down_all + bound_x * phase_field
    y_term = periodic_term(phase_field, 2, 6, bound_y)
    z_term = periodic_term(phase_field, 3, 5, bound_z)
    stream = x_term + y_term + z_term
    advected = phase_field - nu_step * thermal_speed.reshape(own_count, 1, 1, 1, 1, 1, 1) * stream

    low_all = spread
    for _, got in shift_permutes(spread, "mode", holders, mode_devs, False):
        low_all = low_all + got
    low_all = low_all.reshape(species_all, low_count, block_cells).astype(jnp.float32)

    chooser = jnp.stack([(pair_kind == k).astype(jnp.float32) for k in range(NKIND)])
    partner = jnp.einsum("ksr,rlc->klsc", chooser, low_all, precision=lax.Precision.HIGHEST)
    part_hi = partner.astype(jnp.bfloat16)
    part_lo = (partner - part_hi.astype(jnp.float32)).astype(jnp.bfloat16)
    rhs = jnp.stack([piece for k in range(NKIND) for piece in (part_hi[k], part_lo[k])])
    rhs = jnp.pad(rhs, ((0, 0), (0, PAD - low_count), (0, 0), (0, 0)))
    rhs = rhs.reshape(2 * NKIND * PAD, species_all * block_cells)
    lmat = jnp.pad(jnp.moveaxis(low_all, 1, 0), ((0, PAD - low_count), (0, 0), (0, 0)))
    lmat = lmat.reshape(PAD, species_all * block_cells)
    kpad = jnp.pad(kernel, ((0, 0), (0, 0), (0, PAD - low_count), (0, PAD - low_count)))
    kcat = jnp.concatenate([kpad[k] for k in range(NKIND) for _ in range(2)], axis=-1)
    gained = collide_call(kcat, rhs, lmat)

    gained = gained.reshape(out_rows, species_devs, 1, own_count, block_cells)
    gained = jnp.broadcast_to(
        gained, (out_rows, species_devs, mode_devs, own_count, block_cells)
    ).reshape(out_rows, species_devs * mode_devs, own_count, block_cells)
    gathered = lax.all_to_all(gained.astype(jnp.bfloat16), ("species", "mode"), 1, 1, tiled=True)
    gathered = gathered.astype(jnp.float32)
    gathered = gathered.reshape(out_rows, species_devs, mode_devs, own_count, block_cells)
    all_gained = jnp.transpose(gathered, (2, 0, 3, 1, 4)).reshape(
        mode_devs * out_rows, own_count, cell_count
    )

    local_modes = mode_id * mode_count + jnp.arange(mode_count)
    match = low_map[None, :] == local_modes[:, None]
    inverse = jnp.argmax(match, axis=1)
    coll_low = jnp.moveaxis(jnp.take(all_gained, inverse, axis=0), 0, 1)
    vx_degree = first_vx + jnp.arange(per_vx)
    degree_total = (
        vx_degree[:, None, None] + jnp.arange(NVY)[None, :, None] + jnp.arange(NVZ)[None, None, :]
    ).reshape(1, mode_count, 1)
    collide = jnp.where(
        degree_total > DEG, -relax_rate.reshape(own_count, 1, 1) * flat_dist, coll_low
    )
    return advected.reshape(
        own_count, mode_count, row_count, plane_cells
    ) + dt_step * collide.reshape(own_count, mode_count, row_count, plane_cells)


def solution(mesh):
    in_specs = (
        P("species", "mode", "space", None),
        P(None, "mode", None, None),
        P(),
        P(),
        P("species"),
        P("species"),
    )
    out_specs = P("species", "mode", "space", None)
    return jax.shard_map(
        per_device, mesh=mesh, in_specs=in_specs, out_specs=out_specs, check_vma=False
    )
```

```python
import jax
import jax.numpy as jnp
from jax import lax
from jax.experimental import pallas as pl
from jax.sharding import PartitionSpec as P

NVY = 8
NVZ = 8
DEG = 7
NKIND = 2
NY = 256
NZ = 2
PAD = 128
ROW_CHUNK = 10

nu_step = 0.0625
dt_step = 0.05
bound_x = 6.7
bound_y = 4.2
bound_z = 4.2

INTERPRET = False


def flux_from_padded(padded, axis_dim, first_degree):
    axis_count = padded.shape[axis_dim] - 2
    dims_shape = [1] * padded.ndim
    dims_shape[axis_dim] = axis_count
    degree = (first_degree + jnp.arange(axis_count)).astype(jnp.float32).reshape(dims_shape)
    below_part = lax.slice_in_dim(padded, 0, axis_count, axis=axis_dim)
    above_part = lax.slice_in_dim(padded, 2, axis_count + 2, axis=axis_dim)
    return jnp.sqrt(degree + 1.0) * above_part + jnp.sqrt(degree) * below_part


def degree_flux(phase_field, axis_dim):
    widths = [(0, 0)] * phase_field.ndim
    widths[axis_dim] = (1, 1)
    return flux_from_padded(jnp.pad(phase_field, widths), axis_dim, 0)


def rusanov(phase_field, up_field, down_field, up_flux, down_flux, speed_bound):
    return 0.5 * (up_flux - down_flux) - 0.5 * speed_bound * (
        up_field - 2.0 * phase_field + down_field
    )


def periodic_term(phase_field, axis_deg, axis_cell, speed_bound):
    flux_dir = degree_flux(phase_field, axis_deg)
    return rusanov(
        phase_field,
        jnp.roll(phase_field, -1, axis_cell),
        jnp.roll(phase_field, 1, axis_cell),
        jnp.roll(flux_dir, -1, axis_cell),
        jnp.roll(flux_dir, 1, axis_cell),
        speed_bound,
    )


def collide_body(k_ref, r_ref, l_ref, o_ref):
    rows, depth, width = k_ref.shape
    chunk = ROW_CHUNK

    def body(step, carry):
        first = step * chunk
        block = k_ref[pl.ds(first, chunk)].reshape(chunk * depth, width)
        z = jnp.dot(block, r_ref[...], preferred_element_type=jnp.float32)
        for i in range(chunk):
            part = z[i * depth : (i + 1) * depth] * l_ref[...]
            o_ref[pl.ds(first + i, 1), :] = jnp.sum(part, axis=0, keepdims=True)
        return carry

    lax.fori_loop(0, rows // chunk, body, 0)


def collide_call(kcat, rhs, lmat):
    return pl.pallas_call(
        collide_body,
        out_shape=jax.ShapeDtypeStruct((kcat.shape[0], rhs.shape[1]), jnp.float32),
        interpret=INTERPRET,
    )(kcat, rhs, lmat)


def shift_permutes(values, axis, holders, count, toward):
    received = []
    for shift in range(1, count):
        if toward:
            pairs = [((h - shift) % count, h) for h in holders]
        else:
            pairs = [(h, (h + shift) % count) for h in holders]
        received.append((shift, lax.ppermute(values, axis, pairs)))
    return received


def per_device(distribution, kernel, pair_kind, low_map, thermal_speed, relax_rate):
    own_count, mode_count, row_count, plane_cells = distribution.shape
    per_vx = mode_count // (NVY * NVZ)
    mode_devs = lax.axis_size("mode")
    species_devs = lax.axis_size("species")
    space_devs = lax.axis_size("space")
    mode_id = lax.axis_index("mode")
    first_vx = mode_id * per_vx
    low_count = low_map.shape[0]
    out_rows = kernel.shape[1]
    species_all = own_count * species_devs

    phase_field = distribution.reshape(own_count, per_vx, NVY, NVZ, row_count, NZ, NY)
    below = lax.ppermute(
        phase_field[:, per_vx - 1 :].astype(jnp.float16),
        "mode",
        [(i, i + 1) for i in range(mode_devs - 1)],
    ).astype(jnp.float32)
    above = lax.ppermute(
        phase_field[:, :1].astype(jnp.float16), "mode", [(i + 1, i) for i in range(mode_devs - 1)]
    ).astype(jnp.float32)
    flux_x = flux_from_padded(jnp.concatenate([below, phase_field, above], axis=1), 1, first_vx)
    up_part = 0.5 * flux_x - 0.5 * bound_x * phase_field
    down_part = -0.5 * flux_x - 0.5 * bound_x * phase_field
    cell_count = row_count * plane_cells
    block_cells = cell_count // species_devs
    flat_dist = distribution.reshape(own_count, mode_count, cell_count)
    local_index = low_map - mode_id * mode_count
    owned = (local_index >= 0) & (local_index < mode_count)
    clipped = jnp.clip(local_index, 0, mode_count - 1)
    picked = jnp.where(owned[None, :, None], jnp.take(flat_dist, clipped, axis=1), 0.0).astype(
        jnp.bfloat16
    )
    picked = picked.reshape(own_count, low_count, species_devs, block_cells)
    spread = lax.all_to_all(picked, "species", 2, 0, tiled=True)
    up_edge = up_part[:, :, :, :, :1].astype(jnp.float16)
    down_edge = down_part[:, :, :, :, row_count - 1 :].astype(jnp.float16)
    up_edge, down_edge, spread = lax.optimization_barrier((up_edge, down_edge, spread))
    from_next = lax.ppermute(
        up_edge, "space", [(i + 1, i) for i in range(space_devs - 1)]
    ).astype(jnp.float32)
    from_prev = lax.ppermute(
        down_edge, "space", [(i, i + 1) for i in range(space_devs - 1)]
    ).astype(jnp.float32)
    holders = [h for h in range(mode_devs) if h * per_vx <= DEG]
    up_all = jnp.concatenate([up_part[:, :, :, :, 1:], from_next], axis=4)
    down_all = jnp.concatenate([from_prev, down_part[:, :, :, :, : row_count - 1]], axis=4)
    x_term = up_all + down_all + bound_x * phase_field
    y_term = periodic_term(phase_field, 2, 6, bound_y)
    z_term = periodic_term(phase_field, 3, 5, bound_z)
    stream = x_term + y_term + z_term
    advected = phase_field - nu_step * thermal_speed.reshape(own_count, 1, 1, 1, 1, 1, 1) * stream

    low_all = spread
    for _, got in shift_permutes(spread, "mode", holders, mode_devs, False):
        low_all = low_all + got
    low_all = low_all.reshape(species_all, low_count, block_cells).astype(jnp.float32)

    chooser = jnp.stack([(pair_kind == k).astype(jnp.float32) for k in range(NKIND)])
    partner = jnp.einsum("ksr,rlc->klsc", chooser, low_all, precision=lax.Precision.HIGHEST)
    part_hi = partner.astype(jnp.bfloat16)
    part_lo = (partner - part_hi.astype(jnp.float32)).astype(jnp.bfloat16)
    rhs = jnp.stack([piece for k in range(NKIND) for piece in (part_hi[k], part_lo[k])])
    rhs = jnp.pad(rhs, ((0, 0), (0, PAD - low_count), (0, 0), (0, 0)))
    rhs = rhs.reshape(2 * NKIND * PAD, species_all * block_cells)
    lmat = jnp.pad(jnp.moveaxis(low_all, 1, 0), ((0, PAD - low_count), (0, 0), (0, 0)))
    lmat = lmat.reshape(PAD, species_all * block_cells)
    kpad = jnp.pad(kernel, ((0, 0), (0, 0), (0, PAD - low_count), (0, PAD - low_count)))
    kcat = jnp.concatenate([kpad[k] for k in range(NKIND) for _ in range(2)], axis=-1)
    gained = collide_call(kcat, rhs, lmat)

    gained = gained.reshape(out_rows, species_devs, 1, own_count, block_cells)
    gained = jnp.broadcast_to(
        gained, (out_rows, species_devs, mode_devs, own_count, block_cells)
    ).reshape(out_rows, species_devs * mode_devs, own_count, block_cells)
    gathered = lax.all_to_all(gained.astype(jnp.bfloat16), ("species", "mode"), 1, 1, tiled=True)
    gathered = gathered.astype(jnp.float32)
    gathered = gathered.reshape(out_rows, species_devs, mode_devs, own_count, block_cells)
    all_gained = jnp.transpose(gathered, (2, 0, 3, 1, 4)).reshape(
        mode_devs * out_rows, own_count, cell_count
    )

    local_modes = mode_id * mode_count + jnp.arange(mode_count)
    match = low_map[None, :] == local_modes[:, None]
    inverse = jnp.argmax(match, axis=1)
    coll_low = jnp.moveaxis(jnp.take(all_gained, inverse, axis=0), 0, 1)
    vx_degree = first_vx + jnp.arange(per_vx)
    degree_total = (
        vx_degree[:, None, None] + jnp.arange(NVY)[None, :, None] + jnp.arange(NVZ)[None, None, :]
    ).reshape(1, mode_count, 1)
    collide = jnp.where(
        degree_total > DEG, -relax_rate.reshape(own_count, 1, 1) * flat_dist, coll_low
    )
    return advected.reshape(
        own_count, mode_count, row_count, plane_cells
    ) + dt_step * collide.reshape(own_count, mode_count, row_count, plane_cells)


def solution(mesh):
    in_specs = (
        P("species", "mode", "space", None),
        P(None, "mode", None, None),
        P(),
        P(),
        P("species"),
        P("species"),
    )
    out_specs = P("species", "mode", "space", None)
    return jax.shard_map(
        per_device, mesh=mesh, in_specs=in_specs, out_specs=out_specs, check_vma=False
    )
```

```python
import jax
import jax.numpy as jnp
from jax import lax
from jax.experimental import pallas as pl
from jax.sharding import PartitionSpec as P

NVY = 8
NVZ = 8
DEG = 7
NKIND = 2
NY = 256
NZ = 2
PAD = 128
ROW_CHUNK = 10

nu_step = 0.0625
dt_step = 0.05
bound_x = 6.7
bound_y = 4.2
bound_z = 4.2

INTERPRET = False


def flux_from_padded(padded, axis_dim, first_degree):
    axis_count = padded.shape[axis_dim] - 2
    dims_shape = [1] * padded.ndim
    dims_shape[axis_dim] = axis_count
    degree = (first_degree + jnp.arange(axis_count)).astype(jnp.float32).reshape(dims_shape)
    below_part = lax.slice_in_dim(padded, 0, axis_count, axis=axis_dim)
    above_part = lax.slice_in_dim(padded, 2, axis_count + 2, axis=axis_dim)
    return jnp.sqrt(degree + 1.0) * above_part + jnp.sqrt(degree) * below_part


def degree_flux(phase_field, axis_dim):
    widths = [(0, 0)] * phase_field.ndim
    widths[axis_dim] = (1, 1)
    return flux_from_padded(jnp.pad(phase_field, widths), axis_dim, 0)


def rusanov(phase_field, up_field, down_field, up_flux, down_flux, speed_bound):
    return 0.5 * (up_flux - down_flux) - 0.5 * speed_bound * (
        up_field - 2.0 * phase_field + down_field
    )


def periodic_term(phase_field, axis_deg, axis_cell, speed_bound):
    flux_dir = degree_flux(phase_field, axis_deg)
    return rusanov(
        phase_field,
        jnp.roll(phase_field, -1, axis_cell),
        jnp.roll(phase_field, 1, axis_cell),
        jnp.roll(flux_dir, -1, axis_cell),
        jnp.roll(flux_dir, 1, axis_cell),
        speed_bound,
    )


def collide_body(k_ref, r_ref, l_ref, o_ref):
    rows, depth, width = k_ref.shape
    chunk = ROW_CHUNK

    def body(step, carry):
        first = step * chunk
        block = k_ref[pl.ds(first, chunk)].reshape(chunk * depth, width)
        z = jnp.dot(block, r_ref[...], preferred_element_type=jnp.float32)
        for i in range(chunk):
            part = z[i * depth : (i + 1) * depth] * l_ref[...]
            o_ref[pl.ds(first + i, 1), :] = jnp.sum(part, axis=0, keepdims=True)
        return carry

    lax.fori_loop(0, rows // chunk, body, 0)


def collide_call(kcat, rhs, lmat):
    return pl.pallas_call(
        collide_body,
        out_shape=jax.ShapeDtypeStruct((kcat.shape[0], rhs.shape[1]), jnp.float32),
        interpret=INTERPRET,
    )(kcat, rhs, lmat)


def shift_permutes(values, axis, holders, count, toward):
    received = []
    for shift in range(1, count):
        if toward:
            pairs = [((h - shift) % count, h) for h in holders]
        else:
            pairs = [(h, (h + shift) % count) for h in holders]
        received.append((shift, lax.ppermute(values, axis, pairs)))
    return received


def per_device(distribution, kernel, pair_kind, low_map, thermal_speed, relax_rate):
    own_count, mode_count, row_count, plane_cells = distribution.shape
    per_vx = mode_count // (NVY * NVZ)
    mode_devs = lax.axis_size("mode")
    species_devs = lax.axis_size("species")
    space_devs = lax.axis_size("space")
    mode_id = lax.axis_index("mode")
    first_vx = mode_id * per_vx
    low_count = low_map.shape[0]
    out_rows = kernel.shape[1]
    species_all = own_count * species_devs

    phase_field = distribution.reshape(own_count, per_vx, NVY, NVZ, row_count, NZ, NY)
    below = lax.ppermute(
        phase_field[:, per_vx - 1 :].astype(jnp.float16),
        "mode",
        [(i, i + 1) for i in range(mode_devs - 1)],
    ).astype(jnp.float32)
    above = lax.ppermute(
        phase_field[:, :1].astype(jnp.float16), "mode", [(i + 1, i) for i in range(mode_devs - 1)]
    ).astype(jnp.float32)
    flux_x = flux_from_padded(jnp.concatenate([below, phase_field, above], axis=1), 1, first_vx)
    up_part = 0.5 * flux_x - 0.5 * bound_x * phase_field
    down_part = -0.5 * flux_x - 0.5 * bound_x * phase_field
    cell_count = row_count * plane_cells
    block_cells = cell_count // species_devs
    flat_dist = distribution.reshape(own_count, mode_count, cell_count)
    local_index = low_map - mode_id * mode_count
    owned = (local_index >= 0) & (local_index < mode_count)
    clipped = jnp.clip(local_index, 0, mode_count - 1)
    picked = jnp.where(owned[None, :, None], jnp.take(flat_dist, clipped, axis=1), 0.0).astype(
        jnp.bfloat16
    )
    picked = picked.reshape(own_count, low_count, species_devs, block_cells)
    spread = lax.all_to_all(picked, "species", 2, 0, tiled=True)
    up_edge = up_part[:, :, :, :, :1].astype(jnp.float16)
    down_edge = down_part[:, :, :, :, row_count - 1 :].astype(jnp.float16)
    up_edge, down_edge, spread = lax.optimization_barrier((up_edge, down_edge, spread))
    from_next = lax.ppermute(
        up_edge, "space", [(i + 1, i) for i in range(space_devs - 1)]
    ).astype(jnp.float32)
    from_prev = lax.ppermute(
        down_edge, "space", [(i, i + 1) for i in range(space_devs - 1)]
    ).astype(jnp.float32)
    holders = [h for h in range(mode_devs) if h * per_vx <= DEG]
    up_all = jnp.concatenate([up_part[:, :, :, :, 1:], from_next], axis=4)
    down_all = jnp.concatenate([from_prev, down_part[:, :, :, :, : row_count - 1]], axis=4)
    y_term = periodic_term(phase_field, 2, 6, bound_y)
    z_term = periodic_term(phase_field, 3, 5, bound_z)
    step_scale = nu_step * thermal_speed.reshape(own_count, 1, 1, 1, 1, 1, 1)
    partial = lax.optimization_barrier(
        phase_field - step_scale * (bound_x * phase_field + y_term + z_term)
    )
    advected = partial - step_scale * (up_all + down_all)

    low_all = spread
    for _, got in shift_permutes(spread, "mode", holders, mode_devs, False):
        low_all = low_all + got
    low_all = low_all.reshape(species_all, low_count, block_cells).astype(jnp.float32)

    chooser = jnp.stack([(pair_kind == k).astype(jnp.float32) for k in range(NKIND)])
    partner = jnp.einsum("ksr,rlc->klsc", chooser, low_all, precision=lax.Precision.HIGHEST)
    part_hi = partner.astype(jnp.bfloat16)
    part_lo = (partner - part_hi.astype(jnp.float32)).astype(jnp.bfloat16)
    rhs = jnp.stack([piece for k in range(NKIND) for piece in (part_hi[k], part_lo[k])])
    rhs = jnp.pad(rhs, ((0, 0), (0, PAD - low_count), (0, 0), (0, 0)))
    rhs = rhs.reshape(2 * NKIND * PAD, species_all * block_cells)
    lmat = jnp.pad(jnp.moveaxis(low_all, 1, 0), ((0, PAD - low_count), (0, 0), (0, 0)))
    lmat = lmat.reshape(PAD, species_all * block_cells)
    kpad = jnp.pad(kernel, ((0, 0), (0, 0), (0, PAD - low_count), (0, PAD - low_count)))
    kcat = jnp.concatenate([kpad[k] for k in range(NKIND) for _ in range(2)], axis=-1)
    gained = collide_call(kcat, rhs, lmat)

    gained = gained.reshape(out_rows, species_devs, 1, own_count, block_cells)
    gained = jnp.broadcast_to(
        gained, (out_rows, species_devs, mode_devs, own_count, block_cells)
    ).reshape(out_rows, species_devs * mode_devs, own_count, block_cells)
    gathered = lax.all_to_all(gained.astype(jnp.bfloat16), ("species", "mode"), 1, 1, tiled=True)
    gathered = gathered.astype(jnp.float32)
    gathered = gathered.reshape(out_rows, species_devs, mode_devs, own_count, block_cells)
    all_gained = jnp.transpose(gathered, (2, 0, 3, 1, 4)).reshape(
        mode_devs * out_rows, own_count, cell_count
    )

    local_modes = mode_id * mode_count + jnp.arange(mode_count)
    match = low_map[None, :] == local_modes[:, None]
    inverse = jnp.argmax(match, axis=1)
    coll_low = jnp.moveaxis(jnp.take(all_gained, inverse, axis=0), 0, 1)
    vx_degree = first_vx + jnp.arange(per_vx)
    degree_total = (
        vx_degree[:, None, None] + jnp.arange(NVY)[None, :, None] + jnp.arange(NVZ)[None, None, :]
    ).reshape(1, mode_count, 1)
    collide = jnp.where(
        degree_total > DEG, -relax_rate.reshape(own_count, 1, 1) * flat_dist, coll_low
    )
    return advected.reshape(
        own_count, mode_count, row_count, plane_cells
    ) + dt_step * collide.reshape(own_count, mode_count, row_count, plane_cells)


def solution(mesh):
    in_specs = (
        P("species", "mode", "space", None),
        P(None, "mode", None, None),
        P(),
        P(),
        P("species"),
        P("species"),
    )
    out_specs = P("species", "mode", "space", None)
    return jax.shard_map(
        per_device, mesh=mesh, in_specs=in_specs, out_specs=out_specs, check_vma=False
    )
```

```python
import jax
import jax.numpy as jnp
from jax import lax
from jax.experimental import pallas as pl
from jax.sharding import PartitionSpec as P

NVY = 8
NVZ = 8
DEG = 7
NKIND = 2
NY = 256
NZ = 2
PAD = 128
ROW_CHUNK = 10

nu_step = 0.0625
dt_step = 0.05
bound_x = 6.7
bound_y = 4.2
bound_z = 4.2

INTERPRET = False


def flux_from_padded(padded, axis_dim, first_degree):
    axis_count = padded.shape[axis_dim] - 2
    dims_shape = [1] * padded.ndim
    dims_shape[axis_dim] = axis_count
    degree = (first_degree + jnp.arange(axis_count)).astype(jnp.float32).reshape(dims_shape)
    below_part = lax.slice_in_dim(padded, 0, axis_count, axis=axis_dim)
    above_part = lax.slice_in_dim(padded, 2, axis_count + 2, axis=axis_dim)
    return jnp.sqrt(degree + 1.0) * above_part + jnp.sqrt(degree) * below_part


def degree_flux(phase_field, axis_dim):
    widths = [(0, 0)] * phase_field.ndim
    widths[axis_dim] = (1, 1)
    return flux_from_padded(jnp.pad(phase_field, widths), axis_dim, 0)


def rusanov(phase_field, up_field, down_field, up_flux, down_flux, speed_bound):
    return 0.5 * (up_flux - down_flux) - 0.5 * speed_bound * (
        up_field - 2.0 * phase_field + down_field
    )


def periodic_term(phase_field, axis_deg, axis_cell, speed_bound):
    flux_dir = degree_flux(phase_field, axis_deg)
    return rusanov(
        phase_field,
        jnp.roll(phase_field, -1, axis_cell),
        jnp.roll(phase_field, 1, axis_cell),
        jnp.roll(flux_dir, -1, axis_cell),
        jnp.roll(flux_dir, 1, axis_cell),
        speed_bound,
    )


def collide_body(k_ref, r_ref, l_ref, o_ref):
    rows, depth, width = k_ref.shape
    chunk = ROW_CHUNK

    def body(step, carry):
        first = step * chunk
        block = k_ref[pl.ds(first, chunk)].reshape(chunk * depth, width)
        z = jnp.dot(block, r_ref[...], preferred_element_type=jnp.float32)
        for i in range(chunk):
            part = z[i * depth : (i + 1) * depth] * l_ref[...]
            o_ref[pl.ds(first + i, 1), :] = jnp.sum(part, axis=0, keepdims=True)
        return carry

    lax.fori_loop(0, rows // chunk, body, 0)


def collide_call(kcat, rhs, lmat):
    return pl.pallas_call(
        collide_body,
        out_shape=jax.ShapeDtypeStruct((kcat.shape[0], rhs.shape[1]), jnp.float32),
        interpret=INTERPRET,
    )(kcat, rhs, lmat)


def shift_permutes(values, axis, holders, count, toward):
    received = []
    for shift in range(1, count):
        if toward:
            pairs = [((h - shift) % count, h) for h in holders]
        else:
            pairs = [(h, (h + shift) % count) for h in holders]
        received.append((shift, lax.ppermute(values, axis, pairs)))
    return received


def per_device(distribution, kernel, pair_kind, low_map, thermal_speed, relax_rate):
    own_count, mode_count, row_count, plane_cells = distribution.shape
    per_vx = mode_count // (NVY * NVZ)
    mode_devs = lax.axis_size("mode")
    species_devs = lax.axis_size("species")
    space_devs = lax.axis_size("space")
    mode_id = lax.axis_index("mode")
    first_vx = mode_id * per_vx
    low_count = low_map.shape[0]
    out_rows = kernel.shape[1]
    species_all = own_count * species_devs

    phase_field = distribution.reshape(own_count, per_vx, NVY, NVZ, row_count, NZ, NY)
    below = lax.ppermute(
        phase_field[:, per_vx - 1 :].astype(jnp.float16),
        "mode",
        [(i, i + 1) for i in range(mode_devs - 1)],
    ).astype(jnp.float32)
    above = lax.ppermute(
        phase_field[:, :1].astype(jnp.float16), "mode", [(i + 1, i) for i in range(mode_devs - 1)]
    ).astype(jnp.float32)
    flux_x = flux_from_padded(jnp.concatenate([below, phase_field, above], axis=1), 1, first_vx)
    up_part = 0.5 * flux_x - 0.5 * bound_x * phase_field
    down_part = -0.5 * flux_x - 0.5 * bound_x * phase_field
    cell_count = row_count * plane_cells
    block_cells = cell_count // species_devs
    flat_dist = distribution.reshape(own_count, mode_count, cell_count)
    local_index = low_map - mode_id * mode_count
    owned = (local_index >= 0) & (local_index < mode_count)
    clipped = jnp.clip(local_index, 0, mode_count - 1)
    picked = jnp.where(owned[None, :, None], jnp.take(flat_dist, clipped, axis=1), 0.0).astype(
        jnp.bfloat16
    )
    picked = picked.reshape(own_count, low_count, species_devs, block_cells)
    spread = lax.all_to_all(picked, "species", 2, 0, tiled=True)
    up_edge = up_part[:, :, :, :, :1].astype(jnp.float16)
    down_edge = down_part[:, :, :, :, row_count - 1 :].astype(jnp.float16)
    up_edge, down_edge, spread = lax.optimization_barrier((up_edge, down_edge, spread))
    from_next = lax.ppermute(
        up_edge, "space", [(i + 1, i) for i in range(space_devs - 1)]
    ).astype(jnp.float32)
    from_prev = lax.ppermute(
        down_edge, "space", [(i, i + 1) for i in range(space_devs - 1)]
    ).astype(jnp.float32)
    holders = [h for h in range(mode_devs) if h * per_vx <= DEG]
    up_all = jnp.concatenate([up_part[:, :, :, :, 1:], from_next], axis=4)
    down_all = jnp.concatenate([from_prev, down_part[:, :, :, :, : row_count - 1]], axis=4)
    x_term = up_all + down_all + bound_x * phase_field
    y_term = periodic_term(phase_field, 2, 6, bound_y)
    z_term = periodic_term(phase_field, 3, 5, bound_z)
    stream = x_term + y_term + z_term
    advected = phase_field - nu_step * thermal_speed.reshape(own_count, 1, 1, 1, 1, 1, 1) * stream

    low_all = spread
    for _, got in shift_permutes(spread, "mode", holders, mode_devs, False):
        low_all = low_all + got
    low_all = low_all.reshape(species_all, low_count, block_cells).astype(jnp.float32)

    chooser = jnp.stack([(pair_kind == k).astype(jnp.float32) for k in range(NKIND)])
    partner = jnp.einsum("ksr,rlc->klsc", chooser, low_all, precision=lax.Precision.HIGHEST)
    rhs = jnp.pad(partner.astype(jnp.bfloat16), ((0, 0), (0, PAD - low_count), (0, 0), (0, 0)))
    rhs = rhs.reshape(NKIND * PAD, species_all * block_cells)
    lmat = jnp.pad(jnp.moveaxis(low_all, 1, 0), ((0, PAD - low_count), (0, 0), (0, 0)))
    lmat = lmat.reshape(PAD, species_all * block_cells)
    kpad = jnp.pad(kernel, ((0, 0), (0, 0), (0, PAD - low_count), (0, PAD - low_count)))
    kcat = jnp.concatenate([kpad[k] for k in range(NKIND)], axis=-1)
    gained = collide_call(kcat, rhs, lmat)

    gained = gained.reshape(out_rows, species_devs, 1, own_count, block_cells)
    gained = jnp.broadcast_to(
        gained, (out_rows, species_devs, mode_devs, own_count, block_cells)
    ).reshape(out_rows, species_devs * mode_devs, own_count, block_cells)
    gathered = lax.all_to_all(gained.astype(jnp.bfloat16), ("species", "mode"), 1, 1, tiled=True)
    gathered = gathered.astype(jnp.float32)
    gathered = gathered.reshape(out_rows, species_devs, mode_devs, own_count, block_cells)
    all_gained = jnp.transpose(gathered, (2, 0, 3, 1, 4)).reshape(
        mode_devs * out_rows, own_count, cell_count
    )

    local_modes = mode_id * mode_count + jnp.arange(mode_count)
    match = low_map[None, :] == local_modes[:, None]
    inverse = jnp.argmax(match, axis=1)
    coll_low = jnp.moveaxis(jnp.take(all_gained, inverse, axis=0), 0, 1)
    vx_degree = first_vx + jnp.arange(per_vx)
    degree_total = (
        vx_degree[:, None, None] + jnp.arange(NVY)[None, :, None] + jnp.arange(NVZ)[None, None, :]
    ).reshape(1, mode_count, 1)
    collide = jnp.where(
        degree_total > DEG, -relax_rate.reshape(own_count, 1, 1) * flat_dist, coll_low
    )
    return advected.reshape(
        own_count, mode_count, row_count, plane_cells
    ) + dt_step * collide.reshape(own_count, mode_count, row_count, plane_cells)


def solution(mesh):
    in_specs = (
        P("species", "mode", "space", None),
        P(None, "mode", None, None),
        P(),
        P(),
        P("species"),
        P("species"),
    )
    out_specs = P("species", "mode", "space", None)
    return jax.shard_map(
        per_device, mesh=mesh, in_specs=in_specs, out_specs=out_specs, check_vma=False
    )
```

```python
import jax
import jax.numpy as jnp
from jax import lax
from jax.experimental import pallas as pl
from jax.sharding import PartitionSpec as P

NVY = 8
NVZ = 8
DEG = 7
NKIND = 2
NY = 256
NZ = 2
PAD = 128
ROW_CHUNK = 10

nu_step = 0.0625
dt_step = 0.05
bound_x = 6.7
bound_y = 4.2
bound_z = 4.2

INTERPRET = False


def flux_from_padded(padded, axis_dim, first_degree):
    axis_count = padded.shape[axis_dim] - 2
    dims_shape = [1] * padded.ndim
    dims_shape[axis_dim] = axis_count
    degree = (first_degree + jnp.arange(axis_count)).astype(jnp.float32).reshape(dims_shape)
    below_part = lax.slice_in_dim(padded, 0, axis_count, axis=axis_dim)
    above_part = lax.slice_in_dim(padded, 2, axis_count + 2, axis=axis_dim)
    return jnp.sqrt(degree + 1.0) * above_part + jnp.sqrt(degree) * below_part


def degree_flux(phase_field, axis_dim):
    widths = [(0, 0)] * phase_field.ndim
    widths[axis_dim] = (1, 1)
    return flux_from_padded(jnp.pad(phase_field, widths), axis_dim, 0)


def rusanov(phase_field, up_field, down_field, up_flux, down_flux, speed_bound):
    return 0.5 * (up_flux - down_flux) - 0.5 * speed_bound * (
        up_field - 2.0 * phase_field + down_field
    )


def periodic_term(phase_field, axis_deg, axis_cell, speed_bound):
    flux_dir = degree_flux(phase_field, axis_deg)
    return rusanov(
        phase_field,
        jnp.roll(phase_field, -1, axis_cell),
        jnp.roll(phase_field, 1, axis_cell),
        jnp.roll(flux_dir, -1, axis_cell),
        jnp.roll(flux_dir, 1, axis_cell),
        speed_bound,
    )


def collide_body(k_ref, r_ref, l_ref, o_ref):
    rows, depth, width = k_ref.shape
    chunk = ROW_CHUNK

    def body(step, carry):
        first = step * chunk
        block = k_ref[pl.ds(first, chunk)].reshape(chunk * depth, width)
        z = jnp.dot(block, r_ref[...], preferred_element_type=jnp.float32)
        for i in range(chunk):
            part = z[i * depth : (i + 1) * depth] * l_ref[...]
            o_ref[pl.ds(first + i, 1), :] = jnp.sum(part, axis=0, keepdims=True)
        return carry

    lax.fori_loop(0, rows // chunk, body, 0)


def collide_call(kcat, rhs, lmat):
    return pl.pallas_call(
        collide_body,
        out_shape=jax.ShapeDtypeStruct((kcat.shape[0], rhs.shape[1]), jnp.float32),
        interpret=INTERPRET,
    )(kcat, rhs, lmat)


def shift_permutes(values, axis, holders, count, toward):
    received = []
    for shift in range(1, count):
        if toward:
            pairs = [((h - shift) % count, h) for h in holders]
        else:
            pairs = [(h, (h + shift) % count) for h in holders]
        received.append((shift, lax.ppermute(values, axis, pairs)))
    return received


def per_device(distribution, kernel, pair_kind, low_map, thermal_speed, relax_rate):
    own_count, mode_count, row_count, plane_cells = distribution.shape
    per_vx = mode_count // (NVY * NVZ)
    mode_devs = lax.axis_size("mode")
    species_devs = lax.axis_size("species")
    space_devs = lax.axis_size("space")
    mode_id = lax.axis_index("mode")
    first_vx = mode_id * per_vx
    low_count = low_map.shape[0]
    out_rows = kernel.shape[1]
    species_all = own_count * species_devs

    phase_field = distribution.reshape(own_count, per_vx, NVY, NVZ, row_count, NZ, NY)
    below = lax.ppermute(
        phase_field[:, per_vx - 1 :].astype(jnp.float16),
        "mode",
        [(i, i + 1) for i in range(mode_devs - 1)],
    ).astype(jnp.float32)
    above = lax.ppermute(
        phase_field[:, :1].astype(jnp.float16), "mode", [(i + 1, i) for i in range(mode_devs - 1)]
    ).astype(jnp.float32)
    flux_x = flux_from_padded(jnp.concatenate([below, phase_field, above], axis=1), 1, first_vx)
    up_part = 0.5 * flux_x - 0.5 * bound_x * phase_field
    down_part = -0.5 * flux_x - 0.5 * bound_x * phase_field
    cell_count = row_count * plane_cells
    block_cells = cell_count // species_devs
    flat_dist = distribution.reshape(own_count, mode_count, cell_count)
    local_index = low_map - mode_id * mode_count
    owned = (local_index >= 0) & (local_index < mode_count)
    clipped = jnp.clip(local_index, 0, mode_count - 1)
    picked = jnp.where(owned[None, :, None], jnp.take(flat_dist, clipped, axis=1), 0.0).astype(
        jnp.bfloat16
    )
    picked = picked.reshape(own_count, low_count, species_devs, block_cells)
    spread = lax.all_to_all(picked, "species", 2, 0, tiled=True)
    up_edge = up_part[:, :, :, :, :1].astype(jnp.float16)
    down_edge = down_part[:, :, :, :, row_count - 1 :].astype(jnp.float16)
    up_edge, down_edge, spread = lax.optimization_barrier((up_edge, down_edge, spread))
    from_next = lax.ppermute(
        up_edge, "space", [(i + 1, i) for i in range(space_devs - 1)]
    ).astype(jnp.float32)
    from_prev = lax.ppermute(
        down_edge, "space", [(i, i + 1) for i in range(space_devs - 1)]
    ).astype(jnp.float32)
    holders = [h for h in range(mode_devs) if h * per_vx <= DEG]
    up_all = jnp.concatenate([up_part[:, :, :, :, 1:], from_next], axis=4)
    down_all = jnp.concatenate([from_prev, down_part[:, :, :, :, : row_count - 1]], axis=4)

    low_all = spread
    for _, got in shift_permutes(spread, "mode", holders, mode_devs, False):
        low_all = low_all + got
    low_all = low_all.reshape(species_all, low_count, block_cells).astype(jnp.float32)

    chooser = jnp.stack([(pair_kind == k).astype(jnp.float32) for k in range(NKIND)])
    partner = jnp.einsum("ksr,rlc->klsc", chooser, low_all, precision=lax.Precision.HIGHEST)
    part_hi = partner.astype(jnp.bfloat16)
    part_lo = (partner - part_hi.astype(jnp.float32)).astype(jnp.bfloat16)
    rhs = jnp.stack([piece for k in range(NKIND) for piece in (part_hi[k], part_lo[k])])
    rhs = jnp.pad(rhs, ((0, 0), (0, PAD - low_count), (0, 0), (0, 0)))
    rhs = rhs.reshape(2 * NKIND * PAD, species_all * block_cells)
    lmat = jnp.pad(jnp.moveaxis(low_all, 1, 0), ((0, PAD - low_count), (0, 0), (0, 0)))
    lmat = lmat.reshape(PAD, species_all * block_cells)
    kpad = jnp.pad(kernel, ((0, 0), (0, 0), (0, PAD - low_count), (0, PAD - low_count)))
    kcat = jnp.concatenate([kpad[k] for k in range(NKIND) for _ in range(2)], axis=-1)
    gained = collide_call(kcat, rhs, lmat)

    gained = gained.reshape(out_rows, species_devs, 1, own_count, block_cells)
    gained = jnp.broadcast_to(
        gained, (out_rows, species_devs, mode_devs, own_count, block_cells)
    ).reshape(out_rows, species_devs * mode_devs, own_count, block_cells)
    gathered = lax.all_to_all(gained.astype(jnp.bfloat16), ("species", "mode"), 1, 1, tiled=True)
    gathered = gathered.astype(jnp.float32)
    gathered = gathered.reshape(out_rows, species_devs, mode_devs, own_count, block_cells)
    all_gained = jnp.transpose(gathered, (2, 0, 3, 1, 4)).reshape(
        mode_devs * out_rows, own_count, cell_count
    )

    local_modes = mode_id * mode_count + jnp.arange(mode_count)
    match = low_map[None, :] == local_modes[:, None]
    inverse = jnp.argmax(match, axis=1)
    coll_low = jnp.moveaxis(jnp.take(all_gained, inverse, axis=0), 0, 1)
    vx_degree = first_vx + jnp.arange(per_vx)
    degree_total = (
        vx_degree[:, None, None] + jnp.arange(NVY)[None, :, None] + jnp.arange(NVZ)[None, None, :]
    ).reshape(1, mode_count, 1)
    collide = jnp.where(
        degree_total > DEG, -relax_rate.reshape(own_count, 1, 1) * flat_dist, coll_low
    )
    collide, phase_field = lax.optimization_barrier((collide, phase_field))
    x_term = up_all + down_all + bound_x * phase_field
    y_term = periodic_term(phase_field, 2, 6, bound_y)
    z_term = periodic_term(phase_field, 3, 5, bound_z)
    stream = x_term + y_term + z_term
    advected = phase_field - nu_step * thermal_speed.reshape(own_count, 1, 1, 1, 1, 1, 1) * stream
    return advected.reshape(
        own_count, mode_count, row_count, plane_cells
    ) + dt_step * collide.reshape(own_count, mode_count, row_count, plane_cells)


def solution(mesh):
    in_specs = (
        P("species", "mode", "space", None),
        P(None, "mode", None, None),
        P(),
        P(),
        P("species"),
        P("species"),
    )
    out_specs = P("species", "mode", "space", None)
    return jax.shard_map(
        per_device, mesh=mesh, in_specs=in_specs, out_specs=out_specs, check_vma=False
    )
```

```python
import jax
import jax.numpy as jnp
from jax import lax
from jax.experimental import pallas as pl
from jax.sharding import PartitionSpec as P

NVY = 8
NVZ = 8
DEG = 7
NKIND = 2
NY = 256
NZ = 2
PAD = 128
ROW_CHUNK = 10

nu_step = 0.0625
dt_step = 0.05
bound_x = 6.7
bound_y = 4.2
bound_z = 4.2

INTERPRET = False


def flux_from_padded(padded, axis_dim, first_degree):
    axis_count = padded.shape[axis_dim] - 2
    dims_shape = [1] * padded.ndim
    dims_shape[axis_dim] = axis_count
    degree = (first_degree + jnp.arange(axis_count)).astype(jnp.float32).reshape(dims_shape)
    below_part = lax.slice_in_dim(padded, 0, axis_count, axis=axis_dim)
    above_part = lax.slice_in_dim(padded, 2, axis_count + 2, axis=axis_dim)
    return jnp.sqrt(degree + 1.0) * above_part + jnp.sqrt(degree) * below_part


def degree_flux(phase_field, axis_dim):
    widths = [(0, 0)] * phase_field.ndim
    widths[axis_dim] = (1, 1)
    return flux_from_padded(jnp.pad(phase_field, widths), axis_dim, 0)


def rusanov(phase_field, up_field, down_field, up_flux, down_flux, speed_bound):
    return 0.5 * (up_flux - down_flux) - 0.5 * speed_bound * (
        up_field - 2.0 * phase_field + down_field
    )


def periodic_term(phase_field, axis_deg, axis_cell, speed_bound):
    flux_dir = degree_flux(phase_field, axis_deg)
    return rusanov(
        phase_field,
        jnp.roll(phase_field, -1, axis_cell),
        jnp.roll(phase_field, 1, axis_cell),
        jnp.roll(flux_dir, -1, axis_cell),
        jnp.roll(flux_dir, 1, axis_cell),
        speed_bound,
    )


def collide_body(k_ref, r_ref, l_ref, o_ref):
    rows, depth, width = k_ref.shape
    chunk = ROW_CHUNK

    def body(step, carry):
        first = step * chunk
        block = k_ref[pl.ds(first, chunk)].reshape(chunk * depth, width)
        z = jnp.dot(block, r_ref[...], preferred_element_type=jnp.float32)
        for i in range(chunk):
            part = z[i * depth : (i + 1) * depth] * l_ref[...]
            o_ref[pl.ds(first + i, 1), :] = jnp.sum(part, axis=0, keepdims=True)
        return carry

    lax.fori_loop(0, rows // chunk, body, 0)


def collide_call(kcat, rhs, lmat):
    return pl.pallas_call(
        collide_body,
        out_shape=jax.ShapeDtypeStruct((kcat.shape[0], rhs.shape[1]), jnp.float32),
        interpret=INTERPRET,
    )(kcat, rhs, lmat)


def shift_permutes(values, axis, holders, count, toward):
    received = []
    for shift in range(1, count):
        if toward:
            pairs = [((h - shift) % count, h) for h in holders]
        else:
            pairs = [(h, (h + shift) % count) for h in holders]
        received.append((shift, lax.ppermute(values, axis, pairs)))
    return received


def per_device(distribution, kernel, pair_kind, low_map, thermal_speed, relax_rate):
    own_count, mode_count, row_count, plane_cells = distribution.shape
    per_vx = mode_count // (NVY * NVZ)
    mode_devs = lax.axis_size("mode")
    species_devs = lax.axis_size("species")
    space_devs = lax.axis_size("space")
    mode_id = lax.axis_index("mode")
    first_vx = mode_id * per_vx
    low_count = low_map.shape[0]
    out_rows = kernel.shape[1]
    species_all = own_count * species_devs

    phase_field = distribution.reshape(own_count, per_vx, NVY, NVZ, row_count, NZ, NY)
    below = lax.ppermute(
        phase_field[:, per_vx - 1 :].astype(jnp.float16),
        "mode",
        [(i, i + 1) for i in range(mode_devs - 1)],
    ).astype(jnp.float32)
    above = lax.ppermute(
        phase_field[:, :1].astype(jnp.float16), "mode", [(i + 1, i) for i in range(mode_devs - 1)]
    ).astype(jnp.float32)
    flux_x = flux_from_padded(jnp.concatenate([below, phase_field, above], axis=1), 1, first_vx)
    up_part = 0.5 * flux_x - 0.5 * bound_x * phase_field
    down_part = -0.5 * flux_x - 0.5 * bound_x * phase_field
    cell_count = row_count * plane_cells
    block_cells = cell_count // species_devs
    flat_dist = distribution.reshape(own_count, mode_count, cell_count)
    local_index = low_map - mode_id * mode_count
    owned = (local_index >= 0) & (local_index < mode_count)
    clipped = jnp.clip(local_index, 0, mode_count - 1)
    picked = jnp.where(owned[None, :, None], jnp.take(flat_dist, clipped, axis=1), 0.0).astype(
        jnp.bfloat16
    )
    picked = picked.reshape(own_count, low_count, species_devs, block_cells)
    spread = lax.all_to_all(picked, "species", 2, 0, tiled=True)
    up_edge = up_part[:, :, :, :, :1].astype(jnp.float16)
    down_edge = down_part[:, :, :, :, row_count - 1 :].astype(jnp.float16)
    up_edge, down_edge, spread = lax.optimization_barrier((up_edge, down_edge, spread))
    from_next = lax.ppermute(
        up_edge, "space", [(i + 1, i) for i in range(space_devs - 1)]
    ).astype(jnp.float32)
    from_prev = lax.ppermute(
        down_edge, "space", [(i, i + 1) for i in range(space_devs - 1)]
    ).astype(jnp.float32)
    holders = [h for h in range(mode_devs) if h * per_vx <= DEG]
    up_all = jnp.concatenate([up_part[:, :, :, :, 1:], from_next], axis=4)
    down_all = jnp.concatenate([from_prev, down_part[:, :, :, :, : row_count - 1]], axis=4)
    x_term = up_all + down_all + bound_x * phase_field
    y_term = periodic_term(phase_field, 2, 6, bound_y)
    z_term = periodic_term(phase_field, 3, 5, bound_z)
    stream = x_term + y_term + z_term
    advected = phase_field - nu_step * thermal_speed.reshape(own_count, 1, 1, 1, 1, 1, 1) * stream

    low_all = spread
    for _, got in shift_permutes(spread, "mode", holders, mode_devs, False):
        low_all = low_all + got
    low_all = low_all.reshape(species_all, low_count, block_cells).astype(jnp.float32)

    chooser = jnp.stack([(pair_kind == k).astype(jnp.float32) for k in range(NKIND)])
    partner = jnp.einsum("ksr,rlc->klsc", chooser, low_all, precision=lax.Precision.HIGHEST)
    part_hi = partner.astype(jnp.bfloat16)
    part_lo = (partner - part_hi.astype(jnp.float32)).astype(jnp.bfloat16)
    rhs = jnp.stack([piece for k in range(NKIND) for piece in (part_hi[k], part_lo[k])])
    rhs = jnp.pad(rhs, ((0, 0), (0, PAD - low_count), (0, 0), (0, 0)))
    rhs = rhs.reshape(2 * NKIND * PAD, species_all * block_cells)
    lmat = jnp.pad(jnp.moveaxis(low_all, 1, 0), ((0, PAD - low_count), (0, 0), (0, 0)))
    lmat = lmat.reshape(PAD, species_all * block_cells)
    kpad = jnp.pad(kernel, ((0, 0), (0, 0), (0, PAD - low_count), (0, PAD - low_count)))
    kcat = jnp.concatenate([kpad[k] for k in range(NKIND) for _ in range(2)], axis=-1)
    gained = collide_call(kcat, rhs, lmat)

    gained = gained.astype(jnp.bfloat16).reshape(out_rows, species_devs, own_count, block_cells)
    gathered = lax.all_to_all(gained, "species", 1, 3, tiled=True)
    gathered = gathered.reshape(out_rows, own_count, cell_count)
    pieces = [gathered]
    for _, got in shift_permutes(gathered, "mode", holders, mode_devs, True):
        pieces.append(got)
    stacked = jnp.stack(pieces)
    by_source = jnp.take(stacked, (mode_id - jnp.arange(mode_devs)) % mode_devs, axis=0)
    all_gained = by_source.reshape(mode_devs * out_rows, own_count, cell_count).astype(jnp.float32)

    local_modes = mode_id * mode_count + jnp.arange(mode_count)
    match = low_map[None, :] == local_modes[:, None]
    inverse = jnp.argmax(match, axis=1)
    coll_low = jnp.moveaxis(jnp.take(all_gained, inverse, axis=0), 0, 1)
    vx_degree = first_vx + jnp.arange(per_vx)
    degree_total = (
        vx_degree[:, None, None] + jnp.arange(NVY)[None, :, None] + jnp.arange(NVZ)[None, None, :]
    ).reshape(1, mode_count, 1)
    collide = jnp.where(
        degree_total > DEG, -relax_rate.reshape(own_count, 1, 1) * flat_dist, coll_low
    )
    return advected.reshape(
        own_count, mode_count, row_count, plane_cells
    ) + dt_step * collide.reshape(own_count, mode_count, row_count, plane_cells)


def solution(mesh):
    in_specs = (
        P("species", "mode", "space", None),
        P(None, "mode", None, None),
        P(),
        P(),
        P("species"),
        P("species"),
    )
    out_specs = P("species", "mode", "space", None)
    return jax.shard_map(
        per_device, mesh=mesh, in_specs=in_specs, out_specs=out_specs, check_vma=False
    )
```
